32 devices in a mesh: site: 4 (over y, x), sector: 4 (over z), chan: 2 (over core).
Axes of the slice: x: 2, y: 2, z: 4, core: 2. Of those that a mesh axis runs over, the one named last changes fastest.
Arguments:
- environment: bfloat16 [4, 18, 4, 256, 256], P('site', 'chan', 'sector'), may hold values from -6 to 6
- ket_tensor: bfloat16 [4, 4, 4, 256, 256], P('site', 'sector'), may hold values from -0.375 to 0.375
- bra_tensor: bfloat16 [4, 4, 4, 256, 256], P('site', 'sector'), may hold values from -0.375 to 0.375
- mpo_tensor: bfloat16 [4, 18, 18, 4], P('site', None, 'chan'), may hold values from -1.5 to 1.5
- block_length: int32 [4], P('sector'), may hold values from 64 to 256, as said below
Outputs:
- advanced: bfloat16 [4, 18, 4, 256, 256], P('site', 'chan', 'sector')
The draws below stay inside these ranges and needn't reach their ends.
Inputs may be any that keep to these rules, and one draw needn't show every extreme that they name: `block_length`: rows and columns of a sector's block at or past its length are padding: environment's entries there are taken as zero and advanced's entries there are zero; some sector has exactly 256.
All inputs are finite; a program needn't handle non-finite values.
Results may differ from the reference program's by a relative error of at most 0.009.
Values may be sent and summed in bfloat16 or wider, within the bound.
No kernel may reach another device: no remote copies, remote signals or barrier semaphores. Data moves between devices by JAX's collectives and lax.ppermute only.
A program may use at most 64 MiB of HBM per device.

```python
import jax
import jax.numpy as jnp
from jax import lax

BLK = 256
CH = 18
PHYS = 4
STEPS = 2
SITES = 4
SECTORS = 4
STRIDE = 2


def draw_block_length(key, part):
    values = jax.random.randint(jax.random.fold_in(key, 11), (SECTORS,), BLK // 4, BLK + 1)
    where = jax.random.randint(jax.random.fold_in(key, 12), (), 0, SECTORS)
    return jnp.where(jnp.arange(SECTORS) == where, BLK, values).astype(jnp.int32)


def block_levels(stream_key, shape, split, least, largest):
    factor_of, own = 1.0, jax.random.fold_in(stream_key, 6)
    for dim, blocks in split:
        heights = jnp.exp(jax.random.uniform(jax.random.fold_in(own, dim), (blocks,), jnp.float32, least / len(split), largest / len(split)))
        factor_of = factor_of * jnp.repeat(heights, shape[dim] // blocks).reshape([-1 if axis == dim else 1 for axis in range(len(shape))])
    return factor_of


def bell_draw(own_key, dims, scale, limit, shards=(), held_as=jnp.bfloat16):
    loudness = block_levels(own_key, dims, shards, -0.22, 0.18) if shards else 1.0
    array = jax.random.normal(own_key, dims, jnp.float32) * scale * loudness
    return jnp.minimum(jnp.maximum(array, -limit), limit).astype(held_as)


def setup_inputs(seed: int = 0) -> dict:
    splits = jax.random.split(jax.random.key(seed), 6)
    environment = bell_draw(splits[0], (SITES, CH, SECTORS, BLK, BLK), 1.0, 6.0, ((0, 4), (1, 2), (2, 4)))
    ket_tensor = bell_draw(splits[1], (SITES, SECTORS, PHYS, BLK, BLK), BLK ** -0.5, 0.375, ((0, 4), (1, 4)))
    bra_tensor = bell_draw(splits[2], (SITES, SECTORS, PHYS, BLK, BLK), BLK ** -0.5, 0.375, ((0, 4), (1, 4)))
    mpo_tensor = bell_draw(splits[3], (SITES, CH, CH, PHYS), CH ** -0.5, 1.5, ((0, 4), (2, 2)))
    block_length = draw_block_length(jax.random.fold_in(splits[5], 71), 0)
    return {"environment": environment, "ket_tensor": ket_tensor, "bra_tensor": bra_tensor, "mpo_tensor": mpo_tensor, "block_length": block_length}


def reference(environment, ket_tensor, bra_tensor, mpo_tensor, block_length):
    offsets = (0, 1, STRIDE, STRIDE + 1)
    index = jnp.arange(BLK, dtype=jnp.int32)
    alive = index[None, :] < block_length[:, None].astype(jnp.int32)
    live_mask = (alive[:, :, None] & alive[:, None, :]).astype(jnp.float32)

    def advance(operands):
        env_site, ket_site, bra_site, mpo_site = operands
        mixed = jnp.einsum('wvp,wqba->vqpba', mpo_site.astype(jnp.float32), env_site.astype(jnp.float32)).astype(jnp.bfloat16)
        rotated = jnp.einsum('vqpba,qpac->vqpbc', mixed.astype(jnp.float32), ket_site.astype(jnp.float32)).astype(jnp.bfloat16)
        projected = jnp.einsum('qpbd,vqpbc->vqpdc', bra_site.astype(jnp.float32), rotated.astype(jnp.float32)).astype(jnp.bfloat16)
        total = jnp.zeros(env_site.shape, jnp.float32)
        for state in range(PHYS):
            total = total + jnp.roll(projected[:, :, state].astype(jnp.float32), offsets[state], axis=1)
        return (total * live_mask[None]).astype(jnp.bfloat16)

    current = (environment.astype(jnp.float32) * live_mask[None, None]).astype(jnp.bfloat16)
    for step in range(STEPS):
        updated = lax.map(advance, (current, ket_tensor, bra_tensor, mpo_tensor))
        current = jnp.roll(updated, 1, axis=0)
    return current
```

```python
import jax
import jax.numpy as jnp
from jax import lax
from jax.sharding import PartitionSpec as P

STEPS = 2

LINE_P = ((3, 1, 3, 1), (2, 3, 1, 2), (1, 2, 2, 3))
RIGHT = ((0, 1), (1, 2), (2, 3))
LEFT = ((3, 2), (2, 1), (1, 0))
MIDDLE = ((0, 2), (3, 1))
LAST = ((0, 1), (1, 3), (3, 2), (2, 0))


def shifted(value, axis, steps):
    count = lax.axis_size(axis)
    pairs = [(source, (source + steps) % count) for source in range(count)]
    return lax.ppermute(value, axis, pairs)


def term(gathered, ket_p, bra_p, mpo_p):
    mixed = jnp.einsum(
        "wv,wba->vba", mpo_p, gathered, preferred_element_type=jnp.float32
    ).astype(jnp.bfloat16)
    rotated = jnp.einsum(
        "vba,ac->vbc", mixed, ket_p, preferred_element_type=jnp.float32
    ).astype(jnp.bfloat16)
    return jnp.einsum(
        "bd,vbc->vdc", bra_p, rotated, preferred_element_type=jnp.float32
    ).astype(jnp.bfloat16)


def pick(table, sector, ket, bra, mpo):
    p = jnp.asarray(table, jnp.int32)[sector]
    return (
        lax.dynamic_index_in_dim(ket, p, 0, keepdims=False),
        lax.dynamic_index_in_dim(bra, p, 0, keepdims=False),
        lax.dynamic_index_in_dim(mpo, p, 2, keepdims=False),
    )


def advance_line(current, ket, bra, mpo, live_mask, sector):
    gathered = lax.all_gather(current, "chan", axis=0, tiled=True)
    f32 = jnp.float32
    one = jnp.ones((), f32)
    zero = jnp.zeros((), f32)
    slots = [term(gathered, *pick(t, sector, ket, bra, mpo)) for t in LINE_P[:2]]
    got_right = lax.ppermute(
        jnp.where(sector == 2, slots[1], slots[0]), "sector", RIGHT
    )
    got_left = lax.ppermute(
        jnp.where(sector == 1, slots[1], slots[0]), "sector", LEFT
    )
    got_middle = lax.ppermute(slots[1], "sector", MIDDLE)
    third = term(gathered, *pick(LINE_P[2], sector, ket, bra, mpo))
    keep_right = jnp.where(sector == 1, zero, one)
    keep_left = jnp.where(sector == 2, zero, one)
    send = third.astype(f32) + (1 - keep_right) * got_right.astype(f32)
    send = send + (1 - keep_left) * got_left.astype(f32)
    got_last = lax.ppermute(send.astype(jnp.bfloat16), "sector", LAST)
    own = term(gathered, ket[0], bra[0], mpo[:, :, 0])
    total = own.astype(f32) + keep_right * got_right.astype(f32)
    total = total + keep_left * got_left.astype(f32)
    total = total + got_middle.astype(f32) + got_last.astype(f32)
    return (total * live_mask[None]).astype(jnp.bfloat16)


def advance_direct(current, ket, bra, mpo, live_mask):
    stride = lax.axis_size("sector") // 2
    gathered = lax.all_gather(current, "chan", axis=0, tiled=True)
    f32 = jnp.float32
    total = term(gathered, ket[0], bra[0], mpo[:, :, 0]).astype(f32)
    for p, steps in ((1, 1), (2, stride), (3, stride + 1)):
        part = term(gathered, ket[p], bra[p], mpo[:, :, p])
        total = total + shifted(part, "sector", steps).astype(f32)
    return (total * live_mask[None]).astype(jnp.bfloat16)


def shards(environment, ket_tensor, bra_tensor, mpo_tensor, block_length):
    width = environment.shape[-1]
    index = jnp.arange(width, dtype=jnp.int32)
    alive = index < block_length[0]
    live_both = alive[:, None] & alive[None, :]
    live_mask = live_both.astype(jnp.float32)
    sector = lax.axis_index("sector")
    line = lax.axis_size("sector") == 4
    tensors = [(ket_tensor[0, 0], bra_tensor[0, 0], mpo_tensor[0])]
    for _ in range(1, STEPS):
        ket, bra, mpo = tensors[-1]
        tensors.append(tuple(shifted(t, "site", -1) for t in (ket, bra, mpo)))
    current = jnp.where(live_both, environment[0, :, 0], jnp.zeros((), jnp.bfloat16))
    for ket, bra, mpo in tensors:
        if line:
            current = advance_line(current, ket, bra, mpo, live_mask, sector)
        else:
            current = advance_direct(current, ket, bra, mpo, live_mask)
    return shifted(current[None, :, None], "site", STEPS)


def solution(mesh):
    return jax.shard_map(
        shards,
        mesh=mesh,
        in_specs=(
            P("site", "chan", "sector", None, None),
            P("site", "sector", None, None, None),
            P("site", "sector", None, None, None),
            P("site", None, "chan", None),
            P("sector"),
        ),
        out_specs=P("site", "chan", "sector", None, None),
        check_vma=False,
    )
```

```python
import jax
import jax.numpy as jnp
from jax import lax
from jax.sharding import PartitionSpec as P

STEPS = 2

SLOT_A = (3, 1, 1, 2)
SLOT_B = (2, 3, 3, 1)
LAST_P = (1, 2, 2, 3)
RIGHT = ((0, 1), (1, 2), (2, 3))
LEFT = ((3, 2), (2, 1), (1, 0))
LAST = ((0, 1), (1, 3), (3, 2), (2, 0))


def shifted(value, axis, steps):
    count = lax.axis_size(axis)
    pairs = [(source, (source + steps) % count) for source in range(count)]
    return lax.ppermute(value, axis, pairs)


def term(gathered, ket_p, bra_p, mpo_p):
    mixed = jnp.einsum(
        "wv,wba->vba", mpo_p, gathered, preferred_element_type=jnp.float32
    ).astype(jnp.bfloat16)
    rotated = jnp.einsum(
        "vba,ac->vbc", mixed, ket_p, preferred_element_type=jnp.float32
    ).astype(jnp.bfloat16)
    return jnp.einsum(
        "bd,vbc->vdc", bra_p, rotated, preferred_element_type=jnp.float32
    ).astype(jnp.bfloat16)


def pick(table, sector, ket, bra, mpo):
    p = jnp.asarray(table, jnp.int32)[sector]
    return (
        lax.dynamic_index_in_dim(ket, p, 0, keepdims=False),
        lax.dynamic_index_in_dim(bra, p, 0, keepdims=False),
        lax.dynamic_index_in_dim(mpo, p, 2, keepdims=False),
    )


def advance_line(current, ket, bra, mpo, live_mask, sector, held):
    gathered = lax.all_gather(current, "chan", axis=0, tiled=True)
    f32 = jnp.float32
    one = jnp.ones((), f32)
    zero = jnp.zeros((), f32)
    slot_a = term(gathered, *pick(SLOT_A, sector, ket, bra, mpo))
    slot_b = term(gathered, *pick(SLOT_B, sector, ket, bra, mpo))
    got_right = lax.ppermute(slot_a, "sector", RIGHT)
    got_left = lax.ppermute(slot_b, "sector", LEFT)
    got_middle = lax.ppermute(slot_b, "sector", ((0, 2),))
    got_middle = got_middle + lax.ppermute(slot_a, "sector", ((3, 1),))
    got_right, held = lax.optimization_barrier((got_right, held))
    third = term(gathered, *pick(LAST_P, sector, ket, bra, mpo))
    keep_right = jnp.where(sector == 1, zero, one)
    keep_left = jnp.where(sector == 2, zero, one)
    send = third.astype(f32) + (1 - keep_right) * got_right.astype(f32)
    send = send + (1 - keep_left) * got_left.astype(f32)
    got_last = lax.ppermute(send.astype(jnp.bfloat16), "sector", LAST)
    own = term(gathered, ket[0], bra[0], mpo[:, :, 0])
    total = own.astype(f32) + keep_right * got_right.astype(f32)
    total = total + keep_left * got_left.astype(f32)
    total = total + got_middle.astype(f32) + got_last.astype(f32)
    return (total * live_mask[None]).astype(jnp.bfloat16), held


def advance_direct(current, ket, bra, mpo, live_mask):
    stride = lax.axis_size("sector") // 2
    gathered = lax.all_gather(current, "chan", axis=0, tiled=True)
    f32 = jnp.float32
    total = term(gathered, ket[0], bra[0], mpo[:, :, 0]).astype(f32)
    for p, steps in ((1, 1), (2, stride), (3, stride + 1)):
        part = term(gathered, ket[p], bra[p], mpo[:, :, p])
        total = total + shifted(part, "sector", steps).astype(f32)
    return (total * live_mask[None]).astype(jnp.bfloat16)


def shards(environment, ket_tensor, bra_tensor, mpo_tensor, block_length):
    width = environment.shape[-1]
    index = jnp.arange(width, dtype=jnp.int32)
    alive = index < block_length[0]
    live_both = alive[:, None] & alive[None, :]
    live_mask = live_both.astype(jnp.float32)
    sector = lax.axis_index("sector")
    line = lax.axis_size("sector") == 4
    tensors = [(ket_tensor[0, 0], bra_tensor[0, 0], mpo_tensor[0])]
    for _ in range(1, STEPS):
        ket, bra, mpo = tensors[-1]
        tensors.append(tuple(shifted(t, "site", -1) for t in (ket, bra, mpo)))
    current = jnp.where(live_both, environment[0, :, 0], jnp.zeros((), jnp.bfloat16))
    for step in range(STEPS):
        ket, bra, mpo = tensors[step]
        if line:
            current, tensors[step + 1 :] = advance_line(
                current, ket, bra, mpo, live_mask, sector, tensors[step + 1 :]
            )
        else:
            current = advance_direct(current, ket, bra, mpo, live_mask)
    return shifted(current[None, :, None], "site", STEPS)


def solution(mesh):
    return jax.shard_map(
        shards,
        mesh=mesh,
        in_specs=(
            P("site", "chan", "sector", None, None),
            P("site", "sector", None, None, None),
            P("site", "sector", None, None, None),
            P("site", None, "chan", None),
            P("sector"),
        ),
        out_specs=P("site", "chan", "sector", None, None),
        check_vma=False,
    )
```

```python
import jax
import jax.numpy as jnp
from jax import lax
from jax.sharding import PartitionSpec as P

STEPS = 2

SLOT_A = (3, 1, 1, 2)
SLOT_B = (2, 3, 3, 1)
LAST_P = (1, 2, 2, 3)
RIGHT = ((0, 1), (1, 2), (2, 3))
LEFT = ((3, 2), (2, 1), (1, 0))
LAST = ((0, 1), (1, 3), (3, 2), (2, 0))


def shifted(value, axis, steps):
    count = lax.axis_size(axis)
    pairs = [(source, (source + steps) % count) for source in range(count)]
    return lax.ppermute(value, axis, pairs)


def term(gathered, ket_p, bra_p, mpo_p):
    mixed = jnp.einsum(
        "wv,wba->vba", mpo_p, gathered, preferred_element_type=jnp.float32
    ).astype(jnp.bfloat16)
    rotated = jnp.einsum(
        "vba,ac->vbc", mixed, ket_p, preferred_element_type=jnp.float32
    ).astype(jnp.bfloat16)
    return jnp.einsum(
        "bd,vbc->vdc", bra_p, rotated, preferred_element_type=jnp.float32
    ).astype(jnp.bfloat16)


def pick(table, sector, ket, bra, mpo):
    p = jnp.asarray(table, jnp.int32)[sector]
    return (
        lax.dynamic_index_in_dim(ket, p, 0, keepdims=False),
        lax.dynamic_index_in_dim(bra, p, 0, keepdims=False),
        lax.dynamic_index_in_dim(mpo, p, 2, keepdims=False),
    )


def advance_line(current, ket, bra, mpo, live_mask, sector, held):
    gathered = lax.all_gather(current, "chan", axis=0, tiled=True)
    f32 = jnp.float32
    one = jnp.ones((), f32)
    zero = jnp.zeros((), f32)
    slot_a = term(gathered, *pick(SLOT_A, sector, ket, bra, mpo))
    slot_b = term(gathered, *pick(SLOT_B, sector, ket, bra, mpo))
    held, slot_a, slot_b = lax.optimization_barrier((held, slot_a, slot_b))
    middle_right = lax.ppermute(slot_b, "sector", ((0, 2),))
    middle_left = lax.ppermute(slot_a, "sector", ((3, 1),))
    got_right = lax.ppermute(slot_a, "sector", RIGHT)
    got_left = lax.ppermute(slot_b, "sector", LEFT)
    got = lax.optimization_barrier((got_right, got_left, middle_right, middle_left))
    got_right, got_left, middle_right, middle_left = got
    got_middle = middle_right + middle_left
    third = term(gathered, *pick(LAST_P, sector, ket, bra, mpo))
    keep_right = jnp.where(sector == 1, zero, one)
    keep_left = jnp.where(sector == 2, zero, one)
    send = third.astype(f32) + (1 - keep_right) * got_right.astype(f32)
    send = send + (1 - keep_left) * got_left.astype(f32)
    got_last = lax.ppermute(send.astype(jnp.bfloat16), "sector", LAST)
    own = term(gathered, ket[0], bra[0], mpo[:, :, 0])
    total = own.astype(f32) + keep_right * got_right.astype(f32)
    total = total + keep_left * got_left.astype(f32)
    total = total + got_middle.astype(f32) + got_last.astype(f32)
    return (total * live_mask[None]).astype(jnp.bfloat16), held


def advance_direct(current, ket, bra, mpo, live_mask):
    stride = lax.axis_size("sector") // 2
    gathered = lax.all_gather(current, "chan", axis=0, tiled=True)
    f32 = jnp.float32
    total = term(gathered, ket[0], bra[0], mpo[:, :, 0]).astype(f32)
    for p, steps in ((1, 1), (2, stride), (3, stride + 1)):
        part = term(gathered, ket[p], bra[p], mpo[:, :, p])
        total = total + shifted(part, "sector", steps).astype(f32)
    return (total * live_mask[None]).astype(jnp.bfloat16)


def shards(environment, ket_tensor, bra_tensor, mpo_tensor, block_length):
    width = environment.shape[-1]
    index = jnp.arange(width, dtype=jnp.int32)
    alive = index < block_length[0]
    live_both = alive[:, None] & alive[None, :]
    live_mask = live_both.astype(jnp.float32)
    sector = lax.axis_index("sector")
    line = lax.axis_size("sector") == 4
    tensors = [(ket_tensor[0, 0], bra_tensor[0, 0], mpo_tensor[0])]
    for _ in range(1, STEPS):
        ket, bra, mpo = tensors[-1]
        tensors.append(tuple(shifted(t, "site", -1) for t in (ket, bra, mpo)))
    current = jnp.where(live_both, environment[0, :, 0], jnp.zeros((), jnp.bfloat16))
    for step in range(STEPS):
        ket, bra, mpo = tensors[step]
        if line:
            current, tensors[step + 1 :] = advance_line(
                current, ket, bra, mpo, live_mask, sector, tensors[step + 1 :]
            )
        else:
            current = advance_direct(current, ket, bra, mpo, live_mask)
    return shifted(current[None, :, None], "site", STEPS)


def solution(mesh):
    return jax.shard_map(
        shards,
        mesh=mesh,
        in_specs=(
            P("site", "chan", "sector", None, None),
            P("site", "sector", None, None, None),
            P("site", "sector", None, None, None),
            P("site", None, "chan", None),
            P("sector"),
        ),
        out_specs=P("site", "chan", "sector", None, None),
        check_vma=False,
    )
```

```python
import jax
import jax.numpy as jnp
from jax import lax
from jax.sharding import PartitionSpec as P

STEPS = 2

SLOT_A = (3, 1, 1, 2)
SLOT_B = (2, 3, 3, 1)
LAST_P = (1, 2, 2, 3)
RIGHT = ((0, 1), (1, 2), (2, 3))
LEFT = ((3, 2), (2, 1), (1, 0))
LAST = ((0, 1), (1, 3), (3, 2), (2, 0))


def shifted(value, axis, steps):
    count = lax.axis_size(axis)
    pairs = [(source, (source + steps) % count) for source in range(count)]
    return lax.ppermute(value, axis, pairs)


def term(gathered, ket_p, bra_p, mpo_p):
    mixed = jnp.einsum(
        "wv,wba->vba", mpo_p, gathered, preferred_element_type=jnp.float32
    ).astype(jnp.bfloat16)
    rotated = jnp.einsum(
        "vba,ac->vbc", mixed, ket_p, preferred_element_type=jnp.float32
    ).astype(jnp.bfloat16)
    return jnp.einsum(
        "bd,vbc->vdc", bra_p, rotated, preferred_element_type=jnp.float32
    ).astype(jnp.bfloat16)


def pick(table, sector, ket, bra, mpo):
    p = jnp.asarray(table, jnp.int32)[sector]
    return (
        lax.dynamic_index_in_dim(ket, p, 0, keepdims=False),
        lax.dynamic_index_in_dim(bra, p, 0, keepdims=False),
        lax.dynamic_index_in_dim(mpo, p, 2, keepdims=False),
    )


def advance_line(gathered, ket, bra, mpo, live_mask, sector, held):
    f32 = jnp.float32
    one = jnp.ones((), f32)
    zero = jnp.zeros((), f32)
    slot_a = term(gathered, *pick(SLOT_A, sector, ket, bra, mpo))
    slot_b = term(gathered, *pick(SLOT_B, sector, ket, bra, mpo))
    held, slot_a, slot_b = lax.optimization_barrier((held, slot_a, slot_b))
    middle_right = lax.ppermute(slot_b, "sector", ((0, 2),))
    middle_left = lax.ppermute(slot_a, "sector", ((3, 1),))
    got_right = lax.ppermute(slot_a, "sector", RIGHT)
    got_left = lax.ppermute(slot_b, "sector", LEFT)
    got = lax.optimization_barrier((got_right, got_left, middle_right, middle_left))
    got_right, got_left, middle_right, middle_left = got
    got_middle = middle_right + middle_left
    third = term(gathered, *pick(LAST_P, sector, ket, bra, mpo))
    keep_right = jnp.where(sector == 1, zero, one)
    keep_left = jnp.where(sector == 2, zero, one)
    send = third.astype(f32) + (1 - keep_right) * got_right.astype(f32)
    send = send + (1 - keep_left) * got_left.astype(f32)
    got_last = lax.ppermute(send.astype(jnp.bfloat16), "sector", LAST)
    own = term(gathered, ket[0], bra[0], mpo[:, :, 0])
    total = own.astype(f32) + keep_right * got_right.astype(f32)
    total = total + keep_left * got_left.astype(f32)
    total = total + got_middle.astype(f32) + got_last.astype(f32)
    return (total * live_mask[None]).astype(jnp.bfloat16), held


def advance_direct(gathered, ket, bra, mpo, live_mask, sector, held):
    stride = lax.axis_size("sector") // 2
    f32 = jnp.float32
    total = term(gathered, ket[0], bra[0], mpo[:, :, 0]).astype(f32)
    for p, steps in ((1, 1), (2, stride), (3, stride + 1)):
        part = term(gathered, ket[p], bra[p], mpo[:, :, p])
        total = total + shifted(part, "sector", steps).astype(f32)
    return (total * live_mask[None]).astype(jnp.bfloat16), held


def shards(environment, ket_tensor, bra_tensor, mpo_tensor, block_length):
    width = environment.shape[-1]
    index = jnp.arange(width, dtype=jnp.int32)
    alive = index < block_length[0]
    live_both = alive[:, None] & alive[None, :]
    live_mask = live_both.astype(jnp.float32)
    sector = lax.axis_index("sector")
    tensors = [(ket_tensor[0, 0], bra_tensor[0, 0], mpo_tensor[0])]
    for _ in range(1, STEPS):
        ket, bra, mpo = tensors[-1]
        tensors.append(tuple(shifted(t, "site", -1) for t in (ket, bra, mpo)))
    current = jnp.where(live_both, environment[0, :, 0], jnp.zeros((), jnp.bfloat16))
    advance = advance_line if lax.axis_size("sector") == 4 else advance_direct
    outputs = mpo_tensor.shape[2]
    cut = (outputs + 1) // 2
    chunks = [(0, cut), (cut, outputs)]
    for step in range(STEPS):
        ket, bra, mpo = tensors[step]
        gathered = lax.all_gather(current, "chan", axis=0, tiled=True)
        held = tensors[step + 1 :]
        parts = []
        for low, high in chunks:
            part, held = advance(
                gathered, ket, bra, mpo[:, low:high], live_mask, sector, held
            )
            if step == STEPS - 1:
                part = shifted(part[None, :, None], "site", STEPS)
            parts.append(part)
        tensors[step + 1 :] = held
        if step < STEPS - 1:
            current = jnp.concatenate(parts, axis=0)
    return jnp.concatenate(parts, axis=1)


def solution(mesh):
    return jax.shard_map(
        shards,
        mesh=mesh,
        in_specs=(
            P("site", "chan", "sector", None, None),
            P("site", "sector", None, None, None),
            P("site", "sector", None, None, None),
            P("site", None, "chan", None),
            P("sector"),
        ),
        out_specs=P("site", "chan", "sector", None, None),
        check_vma=False,
    )
```

```python
import jax
import jax.numpy as jnp
from jax import lax
from jax.sharding import PartitionSpec as P

STEPS = 2

SLOT_A = (3, 1, 1, 2)
SLOT_B = (2, 3, 3, 1)
LAST_P = (1, 2, 2, 3)
RIGHT = ((0, 1), (1, 2), (2, 3))
LEFT = ((3, 2), (2, 1), (1, 0))
LAST = ((0, 1), (1, 3), (3, 2), (2, 0))


def shifted(value, axis, steps):
    count = lax.axis_size(axis)
    pairs = [(source, (source + steps) % count) for source in range(count)]
    return lax.ppermute(value, axis, pairs)


def term(halves, ket_p, bra_p, mpo_p):
    mixed = sum(
        jnp.einsum("wv,wba->vba", rows(mpo_p), half, preferred_element_type=jnp.float32)
        for half, rows in halves
    ).astype(jnp.bfloat16)
    rotated = jnp.einsum(
        "vba,ac->vbc", mixed, ket_p, preferred_element_type=jnp.float32
    ).astype(jnp.bfloat16)
    return jnp.einsum(
        "bd,vbc->vdc", bra_p, rotated, preferred_element_type=jnp.float32
    ).astype(jnp.bfloat16)


def chan_halves(current):
    count = lax.axis_size("chan")
    me = lax.axis_index("chan")
    width = current.shape[0]
    halves = []
    for k in range(count):
        held = current if k == 0 else shifted(current, "chan", k)
        start = ((me - k) % count) * width
        rows = lambda m, start=start: lax.dynamic_slice_in_dim(m, start, width, 0)
        halves.append((held, rows))
    return halves


def pick(table, sector, ket, bra, mpo):
    p = jnp.asarray(table, jnp.int32)[sector]
    return (
        lax.dynamic_index_in_dim(ket, p, 0, keepdims=False),
        lax.dynamic_index_in_dim(bra, p, 0, keepdims=False),
        lax.dynamic_index_in_dim(mpo, p, 2, keepdims=False),
    )


def advance_line(current, ket, bra, mpo, live_mask, sector, held):
    gathered = chan_halves(current)
    f32 = jnp.float32
    one = jnp.ones((), f32)
    zero = jnp.zeros((), f32)
    slot_a = term(gathered, *pick(SLOT_A, sector, ket, bra, mpo))
    slot_b = term(gathered, *pick(SLOT_B, sector, ket, bra, mpo))
    held, slot_a, slot_b = lax.optimization_barrier((held, slot_a, slot_b))
    middle_right = lax.ppermute(slot_b, "sector", ((0, 2),))
    middle_left = lax.ppermute(slot_a, "sector", ((3, 1),))
    got_right = lax.ppermute(slot_a, "sector", RIGHT)
    got_left = lax.ppermute(slot_b, "sector", LEFT)
    got = lax.optimization_barrier((got_right, got_left, middle_right, middle_left))
    got_right, got_left, middle_right, middle_left = got
    got_middle = middle_right + middle_left
    third = term(gathered, *pick(LAST_P, sector, ket, bra, mpo))
    keep_right = jnp.where(sector == 1, zero, one)
    keep_left = jnp.where(sector == 2, zero, one)
    send = third.astype(f32) + (1 - keep_right) * got_right.astype(f32)
    send = send + (1 - keep_left) * got_left.astype(f32)
    got_last = lax.ppermute(send.astype(jnp.bfloat16), "sector", LAST)
    own = term(gathered, ket[0], bra[0], mpo[:, :, 0])
    total = own.astype(f32) + keep_right * got_right.astype(f32)
    total = total + keep_left * got_left.astype(f32)
    total = total + got_middle.astype(f32) + got_last.astype(f32)
    return (total * live_mask[None]).astype(jnp.bfloat16), held


def advance_direct(current, ket, bra, mpo, live_mask):
    stride = lax.axis_size("sector") // 2
    gathered = chan_halves(current)
    f32 = jnp.float32
    total = term(gathered, ket[0], bra[0], mpo[:, :, 0]).astype(f32)
    for p, steps in ((1, 1), (2, stride), (3, stride + 1)):
        part = term(gathered, ket[p], bra[p], mpo[:, :, p])
        total = total + shifted(part, "sector", steps).astype(f32)
    return (total * live_mask[None]).astype(jnp.bfloat16)


def shards(environment, ket_tensor, bra_tensor, mpo_tensor, block_length):
    width = environment.shape[-1]
    index = jnp.arange(width, dtype=jnp.int32)
    alive = index < block_length[0]
    live_both = alive[:, None] & alive[None, :]
    live_mask = live_both.astype(jnp.float32)
    sector = lax.axis_index("sector")
    line = lax.axis_size("sector") == 4
    tensors = [(ket_tensor[0, 0], bra_tensor[0, 0], mpo_tensor[0])]
    for _ in range(1, STEPS):
        ket, bra, mpo = tensors[-1]
        tensors.append(tuple(shifted(t, "site", -1) for t in (ket, bra, mpo)))
    current = jnp.where(live_both, environment[0, :, 0], jnp.zeros((), jnp.bfloat16))
    for step in range(STEPS):
        ket, bra, mpo = tensors[step]
        if line:
            current, tensors[step + 1 :] = advance_line(
                current, ket, bra, mpo, live_mask, sector, tensors[step + 1 :]
            )
        else:
            current = advance_direct(current, ket, bra, mpo, live_mask)
    return shifted(current[None, :, None], "site", STEPS)


def solution(mesh):
    return jax.shard_map(
        shards,
        mesh=mesh,
        in_specs=(
            P("site", "chan", "sector", None, None),
            P("site", "sector", None, None, None),
            P("site", "sector", None, None, None),
            P("site", None, "chan", None),
            P("sector"),
        ),
        out_specs=P("site", "chan", "sector", None, None),
        check_vma=False,
    )
```

```python
import jax
import jax.numpy as jnp
from jax import lax
from jax.sharding import PartitionSpec as P

STEPS = 2

SLOT_A = (3, 1, 1, 2)
SLOT_B = (2, 3, 3, 1)
LAST_P = (1, 2, 2, 3)
RIGHT = ((0, 1), (1, 2), (2, 3))
LEFT = ((3, 2), (2, 1), (1, 0))
LAST = ((0, 1), (1, 3), (3, 2), (2, 0))


def shifted(value, axis, steps):
    count = lax.axis_size(axis)
    pairs = [(source, (source + steps) % count) for source in range(count)]
    return lax.ppermute(value, axis, pairs)


def term(gathered, ket_p, bra_p, mpo_p):
    mixed = jnp.einsum(
        "wv,wba->vba", mpo_p, gathered, preferred_element_type=jnp.float32
    ).astype(jnp.bfloat16)
    rotated = jnp.einsum(
        "vba,ac->vbc", mixed, ket_p, preferred_element_type=jnp.float32
    ).astype(jnp.bfloat16)
    return jnp.einsum(
        "bd,vbc->vdc", bra_p, rotated, preferred_element_type=jnp.float32
    ).astype(jnp.bfloat16)


def chan_gathered(current, mpo):
    count = lax.axis_size("chan")
    me = lax.axis_index("chan")
    width = current.shape[0]
    held = [current] + [shifted(current, "chan", k) for k in range(1, count)]
    rows = [(me - k) % count for k in range(count)]
    order = jnp.concatenate([jnp.arange(width) + r * width for r in rows])
    return jnp.concatenate(held, axis=0), jnp.take(mpo, order, axis=0)


def pick(table, sector, ket, bra, mpo):
    p = jnp.asarray(table, jnp.int32)[sector]
    return (
        lax.dynamic_index_in_dim(ket, p, 0, keepdims=False),
        lax.dynamic_index_in_dim(bra, p, 0, keepdims=False),
        lax.dynamic_index_in_dim(mpo, p, 2, keepdims=False),
    )


def advance_line(current, ket, bra, mpo, live_mask, sector, held):
    gathered, mpo = chan_gathered(current, mpo)
    f32 = jnp.float32
    one = jnp.ones((), f32)
    zero = jnp.zeros((), f32)
    slot_a = term(gathered, *pick(SLOT_A, sector, ket, bra, mpo))
    slot_b = term(gathered, *pick(SLOT_B, sector, ket, bra, mpo))
    held, slot_a, slot_b = lax.optimization_barrier((held, slot_a, slot_b))
    middle_right = lax.ppermute(slot_b, "sector", ((0, 2),))
    middle_left = lax.ppermute(slot_a, "sector", ((3, 1),))
    got_right = lax.ppermute(slot_a, "sector", RIGHT)
    got_left = lax.ppermute(slot_b, "sector", LEFT)
    got = lax.optimization_barrier((got_right, got_left, middle_right, middle_left))
    got_right, got_left, middle_right, middle_left = got
    got_middle = middle_right + middle_left
    third = term(gathered, *pick(LAST_P, sector, ket, bra, mpo))
    keep_right = jnp.where(sector == 1, zero, one)
    keep_left = jnp.where(sector == 2, zero, one)
    send = third.astype(f32) + (1 - keep_right) * got_right.astype(f32)
    send = send + (1 - keep_left) * got_left.astype(f32)
    got_last = lax.ppermute(send.astype(jnp.bfloat16), "sector", LAST)
    own = term(gathered, ket[0], bra[0], mpo[:, :, 0])
    total = own.astype(f32) + keep_right * got_right.astype(f32)
    total = total + keep_left * got_left.astype(f32)
    total = total + got_middle.astype(f32) + got_last.astype(f32)
    return (total * live_mask[None]).astype(jnp.bfloat16), held


def advance_direct(current, ket, bra, mpo, live_mask):
    stride = lax.axis_size("sector") // 2
    gathered, mpo = chan_gathered(current, mpo)
    f32 = jnp.float32
    total = term(gathered, ket[0], bra[0], mpo[:, :, 0]).astype(f32)
    for p, steps in ((1, 1), (2, stride), (3, stride + 1)):
        part = term(gathered, ket[p], bra[p], mpo[:, :, p])
        total = total + shifted(part, "sector", steps).astype(f32)
    return (total * live_mask[None]).astype(jnp.bfloat16)


def shards(environment, ket_tensor, bra_tensor, mpo_tensor, block_length):
    width = environment.shape[-1]
    index = jnp.arange(width, dtype=jnp.int32)
    alive = index < block_length[0]
    live_both = alive[:, None] & alive[None, :]
    live_mask = live_both.astype(jnp.float32)
    sector = lax.axis_index("sector")
    line = lax.axis_size("sector") == 4
    tensors = [(ket_tensor[0, 0], bra_tensor[0, 0], mpo_tensor[0])]
    for _ in range(1, STEPS):
        ket, bra, mpo = tensors[-1]
        tensors.append(tuple(shifted(t, "site", -1) for t in (ket, bra, mpo)))
    current = jnp.where(live_both, environment[0, :, 0], jnp.zeros((), jnp.bfloat16))
    for step in range(STEPS):
        ket, bra, mpo = tensors[step]
        if line:
            current, tensors[step + 1 :] = advance_line(
                current, ket, bra, mpo, live_mask, sector, tensors[step + 1 :]
            )
        else:
            current = advance_direct(current, ket, bra, mpo, live_mask)
    return shifted(current[None, :, None], "site", STEPS)


def solution(mesh):
    return jax.shard_map(
        shards,
        mesh=mesh,
        in_specs=(
            P("site", "chan", "sector", None, None),
            P("site", "sector", None, None, None),
            P("site", "sector", None, None, None),
            P("site", None, "chan", None),
            P("sector"),
        ),
        out_specs=P("site", "chan", "sector", None, None),
        check_vma=False,
    )
```

```python
import jax
import jax.numpy as jnp
from jax import lax
from jax.sharding import PartitionSpec as P

STEPS = 2

SLOT_A = (3, 1, 1, 2)
SLOT_B = (2, 3, 3, 1)
LAST_P = (1, 2, 2, 3)
RIGHT = ((0, 1), (1, 2), (2, 3))
LEFT = ((3, 2), (2, 1), (1, 0))
LAST = ((0, 1), (1, 3), (3, 2), (2, 0))


def shifted(value, axis, steps):
    count = lax.axis_size(axis)
    pairs = [(source, (source + steps) % count) for source in range(count)]
    return lax.ppermute(value, axis, pairs)


def term(gathered, ket_p, bra_p, mpo_p):
    mixed = jnp.einsum(
        "wv,wba->vba", mpo_p, gathered, preferred_element_type=jnp.float32
    ).astype(jnp.bfloat16)
    rotated = jnp.einsum(
        "vba,ac->vbc", mixed, ket_p, preferred_element_type=jnp.float32
    ).astype(jnp.bfloat16)
    return jnp.einsum(
        "bd,vbc->vdc", bra_p, rotated, preferred_element_type=jnp.float32
    ).astype(jnp.bfloat16)


def chan_gathered(current, mpo):
    count = lax.axis_size("chan")
    me = lax.axis_index("chan")
    width = current.shape[0]
    held = [current] + [shifted(current, "chan", k) for k in range(1, count)]
    rows = [(me - k) % count for k in range(count)]
    order = jnp.concatenate([jnp.arange(width) + r * width for r in rows])
    return jnp.concatenate(held, axis=0), jnp.take(mpo, order, axis=0)


def pick(table, sector, ket, bra, mpo):
    p = jnp.asarray(table, jnp.int32)[sector]
    return (
        lax.dynamic_index_in_dim(ket, p, 0, keepdims=False),
        lax.dynamic_index_in_dim(bra, p, 0, keepdims=False),
        lax.dynamic_index_in_dim(mpo, p, 2, keepdims=False),
    )


def advance_line(current, ket, bra, mpo, live_mask, sector, held, pieces, finish):
    gathered, mpo = chan_gathered(current, mpo)
    f32 = jnp.float32
    one = jnp.ones((), f32)
    zero = jnp.zeros((), f32)
    slot_a = term(gathered, *pick(SLOT_A, sector, ket, bra, mpo))
    slot_b = term(gathered, *pick(SLOT_B, sector, ket, bra, mpo))
    held, slot_a, slot_b = lax.optimization_barrier((held, slot_a, slot_b))
    middle_right = lax.ppermute(slot_b, "sector", ((0, 2),))
    middle_left = lax.ppermute(slot_a, "sector", ((3, 1),))
    got_right = lax.ppermute(slot_a, "sector", RIGHT)
    got_left = lax.ppermute(slot_b, "sector", LEFT)
    got = lax.optimization_barrier((got_right, got_left, middle_right, middle_left))
    got_right, got_left, middle_right, middle_left = got
    got_middle = middle_right + middle_left
    third = term(gathered, *pick(LAST_P, sector, ket, bra, mpo))
    keep_right = jnp.where(sector == 1, zero, one)
    keep_left = jnp.where(sector == 2, zero, one)
    send = third.astype(f32) + (1 - keep_right) * got_right.astype(f32)
    send = send + (1 - keep_left) * got_left.astype(f32)
    send = send.astype(jnp.bfloat16)
    own = term(gathered, ket[0], bra[0], mpo[:, :, 0])
    total = own.astype(f32) + keep_right * got_right.astype(f32)
    total = total + keep_left * got_left.astype(f32) + got_middle.astype(f32)
    width = send.shape[0]
    bounds = [width * k // pieces for k in range(pieces + 1)]
    results = []
    piece = None
    for low, high in zip(bounds[:-1], bounds[1:]):
        if results:
            piece, send = lax.optimization_barrier((piece, send))
            results[-1] = finish(piece)
        got_last = lax.ppermute(send[low:high], "sector", LAST)
        if results:
            results[-1], got_last = lax.optimization_barrier((results[-1], got_last))
        piece = total[low:high] + got_last.astype(f32)
        piece = (piece * live_mask[None]).astype(jnp.bfloat16)
        results.append(None)
    results[-1] = finish(piece)
    return results, held


def advance_direct(current, ket, bra, mpo, live_mask):
    stride = lax.axis_size("sector") // 2
    gathered, mpo = chan_gathered(current, mpo)
    f32 = jnp.float32
    total = term(gathered, ket[0], bra[0], mpo[:, :, 0]).astype(f32)
    for p, steps in ((1, 1), (2, stride), (3, stride + 1)):
        part = term(gathered, ket[p], bra[p], mpo[:, :, p])
        total = total + shifted(part, "sector", steps).astype(f32)
    return (total * live_mask[None]).astype(jnp.bfloat16)


def shards(environment, ket_tensor, bra_tensor, mpo_tensor, block_length):
    width = environment.shape[-1]
    index = jnp.arange(width, dtype=jnp.int32)
    alive = index < block_length[0]
    live_both = alive[:, None] & alive[None, :]
    live_mask = live_both.astype(jnp.float32)
    sector = lax.axis_index("sector")
    line = lax.axis_size("sector") == 4
    tensors = [(ket_tensor[0, 0], bra_tensor[0, 0], mpo_tensor[0])]
    for _ in range(1, STEPS):
        ket, bra, mpo = tensors[-1]
        tensors.append(tuple(shifted(t, "site", -1) for t in (ket, bra, mpo)))
    current = jnp.where(live_both, environment[0, :, 0], jnp.zeros((), jnp.bfloat16))
    def onward(part):
        return shifted(part[None, :, None], "site", STEPS)

    for step in range(STEPS):
        ket, bra, mpo = tensors[step]
        last = step == STEPS - 1
        if line:
            parts, tensors[step + 1 :] = advance_line(
                current, ket, bra, mpo, live_mask, sector, tensors[step + 1 :],
                2 if last else 1, onward if last else (lambda part: part),
            )
        else:
            parts = [advance_direct(current, ket, bra, mpo, live_mask)]
            parts = [onward(parts[0])] if last else parts
        if not last:
            current = jnp.concatenate(parts, axis=0)
    return jnp.concatenate(parts, axis=1)


def solution(mesh):
    return jax.shard_map(
        shards,
        mesh=mesh,
        in_specs=(
            P("site", "chan", "sector", None, None),
            P("site", "sector", None, None, None),
            P("site", "sector", None, None, None),
            P("site", None, "chan", None),
            P("sector"),
        ),
        out_specs=P("site", "chan", "sector", None, None),
        check_vma=False,
    )
```

```python
import jax
import jax.numpy as jnp
from jax import lax
from jax.sharding import PartitionSpec as P

STEPS = 2

SLOT_A = (3, 1, 1, 2)
SLOT_B = (2, 3, 3, 1)
LAST_P = (1, 2, 2, 3)
RIGHT = ((0, 1), (1, 2), (2, 3))
LEFT = ((3, 2), (2, 1), (1, 0))
LAST = ((0, 1), (1, 3), (3, 2), (2, 0))


def shifted(value, axis, steps):
    count = lax.axis_size(axis)
    pairs = [(source, (source + steps) % count) for source in range(count)]
    return lax.ppermute(value, axis, pairs)


def term(gathered, ket_p, bra_p, mpo_p):
    mixed = jnp.einsum(
        "wv,wba->vba", mpo_p, gathered, preferred_element_type=jnp.float32
    ).astype(jnp.bfloat16)
    rotated = jnp.einsum(
        "vba,ac->vbc", mixed, ket_p, preferred_element_type=jnp.float32
    ).astype(jnp.bfloat16)
    return jnp.einsum(
        "bd,vbc->vdc", bra_p, rotated, preferred_element_type=jnp.float32
    ).astype(jnp.bfloat16)


def chan_gathered(current, mpo):
    count = lax.axis_size("chan")
    me = lax.axis_index("chan")
    width = current.shape[0]
    held = [current] + [shifted(current, "chan", k) for k in range(1, count)]
    rows = [(me - k) % count for k in range(count)]
    order = jnp.concatenate([jnp.arange(width) + r * width for r in rows])
    return jnp.concatenate(held, axis=0), jnp.take(mpo, order, axis=0)


def pick(table, sector, ket, bra, mpo):
    p = jnp.asarray(table, jnp.int32)[sector]
    return (
        lax.dynamic_index_in_dim(ket, p, 0, keepdims=False),
        lax.dynamic_index_in_dim(bra, p, 0, keepdims=False),
        lax.dynamic_index_in_dim(mpo, p, 2, keepdims=False),
    )


def advance_line(current, ket, bra, mpo, live_mask, sector, held, pieces, finish):
    gathered, mpo = chan_gathered(current, mpo)
    f32 = jnp.float32
    one = jnp.ones((), f32)
    zero = jnp.zeros((), f32)
    slot_a = term(gathered, *pick(SLOT_A, sector, ket, bra, mpo))
    held, slot_a = lax.optimization_barrier((held, slot_a))
    got_right = lax.ppermute(slot_a, "sector", RIGHT)
    middle_left = lax.ppermute(slot_a, "sector", ((3, 1),))
    slot_b = term(gathered, *pick(SLOT_B, sector, ket, bra, mpo))
    got_left = lax.ppermute(slot_b, "sector", LEFT)
    middle_right = lax.ppermute(slot_b, "sector", ((0, 2),))
    got = lax.optimization_barrier((got_right, got_left, middle_right, middle_left))
    got_right, got_left, middle_right, middle_left = got
    got_middle = middle_right + middle_left
    third = term(gathered, *pick(LAST_P, sector, ket, bra, mpo))
    keep_right = jnp.where(sector == 1, zero, one)
    keep_left = jnp.where(sector == 2, zero, one)
    send = third.astype(f32) + (1 - keep_right) * got_right.astype(f32)
    send = send + (1 - keep_left) * got_left.astype(f32)
    send = send.astype(jnp.bfloat16)
    own = term(gathered, ket[0], bra[0], mpo[:, :, 0])
    total = own.astype(f32) + keep_right * got_right.astype(f32)
    total = total + keep_left * got_left.astype(f32) + got_middle.astype(f32)
    width = send.shape[0]
    bounds = [width * k // pieces for k in range(pieces + 1)]
    results = []
    piece = None
    for low, high in zip(bounds[:-1], bounds[1:]):
        if results:
            piece, send = lax.optimization_barrier((piece, send))
            results[-1] = finish(piece)
        got_last = lax.ppermute(send[low:high], "sector", LAST)
        if results:
            results[-1], got_last = lax.optimization_barrier((results[-1], got_last))
        piece = total[low:high] + got_last.astype(f32)
        piece = (piece * live_mask[None]).astype(jnp.bfloat16)
        results.append(None)
    results[-1] = finish(piece)
    return results, held


def advance_direct(current, ket, bra, mpo, live_mask):
    stride = lax.axis_size("sector") // 2
    gathered, mpo = chan_gathered(current, mpo)
    f32 = jnp.float32
    total = term(gathered, ket[0], bra[0], mpo[:, :, 0]).astype(f32)
    for p, steps in ((1, 1), (2, stride), (3, stride + 1)):
        part = term(gathered, ket[p], bra[p], mpo[:, :, p])
        total = total + shifted(part, "sector", steps).astype(f32)
    return (total * live_mask[None]).astype(jnp.bfloat16)


def shards(environment, ket_tensor, bra_tensor, mpo_tensor, block_length):
    width = environment.shape[-1]
    index = jnp.arange(width, dtype=jnp.int32)
    alive = index < block_length[0]
    live_both = alive[:, None] & alive[None, :]
    live_mask = live_both.astype(jnp.float32)
    sector = lax.axis_index("sector")
    line = lax.axis_size("sector") == 4
    tensors = [(ket_tensor[0, 0], bra_tensor[0, 0], mpo_tensor[0])]
    for _ in range(1, STEPS):
        ket, bra, mpo = tensors[-1]
        tensors.append(tuple(shifted(t, "site", -1) for t in (ket, bra, mpo)))
    current = jnp.where(live_both, environment[0, :, 0], jnp.zeros((), jnp.bfloat16))
    def onward(part):
        return shifted(part[None, :, None], "site", STEPS)

    for step in range(STEPS):
        ket, bra, mpo = tensors[step]
        last = step == STEPS - 1
        if line:
            parts, tensors[step + 1 :] = advance_line(
                current, ket, bra, mpo, live_mask, sector, tensors[step + 1 :],
                2 if last else 1, onward if last else (lambda part: part),
            )
        else:
            parts = [advance_direct(current, ket, bra, mpo, live_mask)]
            parts = [onward(parts[0])] if last else parts
        if not last:
            current = jnp.concatenate(parts, axis=0)
    return jnp.concatenate(parts, axis=1)


def solution(mesh):
    return jax.shard_map(
        shards,
        mesh=mesh,
        in_specs=(
            P("site", "chan", "sector", None, None),
            P("site", "sector", None, None, None),
            P("site", "sector", None, None, None),
            P("site", None, "chan", None),
            P("sector"),
        ),
        out_specs=P("site", "chan", "sector", None, None),
        check_vma=False,
    )
```

```python
import jax
import jax.numpy as jnp
from jax import lax
from jax.sharding import PartitionSpec as P

STEPS = 2

SLOT_A = (3, 1, 1, 2)
SLOT_B = (2, 3, 3, 1)
LAST_P = (1, 2, 2, 3)
RIGHT = ((0, 1), (1, 2), (2, 3))
LEFT = ((3, 2), (2, 1), (1, 0))
LAST = ((0, 1), (1, 3), (3, 2), (2, 0))


def shifted(value, axis, steps):
    count = lax.axis_size(axis)
    pairs = [(source, (source + steps) % count) for source in range(count)]
    return lax.ppermute(value, axis, pairs)


def term(gathered, ket_p, bra_p, mpo_p):
    mixed = jnp.einsum(
        "wv,wba->vba", mpo_p, gathered, preferred_element_type=jnp.float32
    ).astype(jnp.bfloat16)
    rotated = jnp.einsum(
        "vba,ac->vbc", mixed, ket_p, preferred_element_type=jnp.float32
    ).astype(jnp.bfloat16)
    return jnp.einsum(
        "bd,vbc->vdc", bra_p, rotated, preferred_element_type=jnp.float32
    ).astype(jnp.bfloat16)


def chan_gathered(current, mpo):
    count = lax.axis_size("chan")
    me = lax.axis_index("chan")
    width = current.shape[0]
    held = [current] + [shifted(current, "chan", k) for k in range(1, count)]
    rows = [(me - k) % count for k in range(count)]
    order = jnp.concatenate([jnp.arange(width) + r * width for r in rows])
    return jnp.concatenate(held, axis=0), jnp.take(mpo, order, axis=0)


def pick(table, sector, ket, bra, mpo):
    p = jnp.asarray(table, jnp.int32)[sector]
    return (
        lax.dynamic_index_in_dim(ket, p, 0, keepdims=False),
        lax.dynamic_index_in_dim(bra, p, 0, keepdims=False),
        lax.dynamic_index_in_dim(mpo, p, 2, keepdims=False),
    )


def advance_line(current, ket, bra, mpo, live_mask, sector, held, pieces, finish):
    gathered, mpo = chan_gathered(current, mpo)
    f32 = jnp.float32
    one = jnp.ones((), f32)
    zero = jnp.zeros((), f32)
    slot_a = term(gathered, *pick(SLOT_A, sector, ket, bra, mpo))
    held, slot_a = lax.optimization_barrier((held, slot_a))
    got_right = lax.ppermute(slot_a, "sector", RIGHT)
    middle_left = lax.ppermute(slot_a, "sector", ((3, 1),))
    slot_b = term(gathered, *pick(SLOT_B, sector, ket, bra, mpo))
    got_left = lax.ppermute(slot_b, "sector", LEFT)
    middle_right = lax.ppermute(slot_b, "sector", ((0, 2),))
    third = term(gathered, *pick(LAST_P, sector, ket, bra, mpo))
    got = (got_right, got_left, middle_right, middle_left, third)
    got_right, got_left, middle_right, middle_left, third = lax.optimization_barrier(got)
    got_middle = middle_right + middle_left
    keep_right = jnp.where(sector == 1, zero, one)
    keep_left = jnp.where(sector == 2, zero, one)
    send = third.astype(f32) + (1 - keep_right) * got_right.astype(f32)
    send = send + (1 - keep_left) * got_left.astype(f32)
    send = send.astype(jnp.bfloat16)
    own = term(gathered, ket[0], bra[0], mpo[:, :, 0])
    total = own.astype(f32) + keep_right * got_right.astype(f32)
    total = total + keep_left * got_left.astype(f32) + got_middle.astype(f32)
    width = send.shape[0]
    bounds = [width * k // pieces for k in range(pieces + 1)]
    results = []
    piece = None
    for low, high in zip(bounds[:-1], bounds[1:]):
        if results:
            piece, send = lax.optimization_barrier((piece, send))
            results[-1] = finish(piece)
        got_last = lax.ppermute(send[low:high], "sector", LAST)
        if results:
            results[-1], got_last = lax.optimization_barrier((results[-1], got_last))
        piece = total[low:high] + got_last.astype(f32)
        piece = (piece * live_mask[None]).astype(jnp.bfloat16)
        results.append(None)
    results[-1] = finish(piece)
    return results, held


def advance_direct(current, ket, bra, mpo, live_mask):
    stride = lax.axis_size("sector") // 2
    gathered, mpo = chan_gathered(current, mpo)
    f32 = jnp.float32
    total = term(gathered, ket[0], bra[0], mpo[:, :, 0]).astype(f32)
    for p, steps in ((1, 1), (2, stride), (3, stride + 1)):
        part = term(gathered, ket[p], bra[p], mpo[:, :, p])
        total = total + shifted(part, "sector", steps).astype(f32)
    return (total * live_mask[None]).astype(jnp.bfloat16)


def shards(environment, ket_tensor, bra_tensor, mpo_tensor, block_length):
    width = environment.shape[-1]
    index = jnp.arange(width, dtype=jnp.int32)
    alive = index < block_length[0]
    live_both = alive[:, None] & alive[None, :]
    live_mask = live_both.astype(jnp.float32)
    sector = lax.axis_index("sector")
    line = lax.axis_size("sector") == 4
    tensors = [(ket_tensor[0, 0], bra_tensor[0, 0], mpo_tensor[0])]
    for _ in range(1, STEPS):
        ket, bra, mpo = tensors[-1]
        tensors.append(tuple(shifted(t, "site", -1) for t in (ket, bra, mpo)))
    current = jnp.where(live_both, environment[0, :, 0], jnp.zeros((), jnp.bfloat16))
    def onward(part):
        return shifted(part[None, :, None], "site", STEPS)

    for step in range(STEPS):
        ket, bra, mpo = tensors[step]
        last = step == STEPS - 1
        if line:
            parts, tensors[step + 1 :] = advance_line(
                current, ket, bra, mpo, live_mask, sector, tensors[step + 1 :],
                2 if last else 1, onward if last else (lambda part: part),
            )
        else:
            parts = [advance_direct(current, ket, bra, mpo, live_mask)]
            parts = [onward(parts[0])] if last else parts
        if not last:
            current = jnp.concatenate(parts, axis=0)
    return jnp.concatenate(parts, axis=1)


def solution(mesh):
    return jax.shard_map(
        shards,
        mesh=mesh,
        in_specs=(
            P("site", "chan", "sector", None, None),
            P("site", "sector", None, None, None),
            P("site", "sector", None, None, None),
            P("site", None, "chan", None),
            P("sector"),
        ),
        out_specs=P("site", "chan", "sector", None, None),
        check_vma=False,
    )
```

```python
import jax
import jax.numpy as jnp
from jax import lax
from jax.sharding import PartitionSpec as P

STEPS = 2

SLOT_A = (3, 1, 1, 2)
SLOT_B = (2, 3, 3, 1)
LAST_P = (1, 2, 2, 3)
RIGHT = ((0, 1), (1, 2), (2, 3))
LEFT = ((3, 2), (2, 1), (1, 0))
LAST = ((0, 1), (1, 3), (3, 2), (2, 0))


def shifted(value, axis, steps):
    count = lax.axis_size(axis)
    pairs = [(source, (source + steps) % count) for source in range(count)]
    return lax.ppermute(value, axis, pairs)


def term(gathered, ket_p, bra_p, mpo_p):
    mixed = jnp.einsum(
        "wv,wba->vba", mpo_p, gathered, preferred_element_type=jnp.float32
    ).astype(jnp.bfloat16)
    rotated = jnp.einsum(
        "vba,ac->vbc", mixed, ket_p, preferred_element_type=jnp.float32
    ).astype(jnp.bfloat16)
    return jnp.einsum(
        "bd,vbc->vdc", bra_p, rotated, preferred_element_type=jnp.float32
    ).astype(jnp.bfloat16)


def chan_gathered(current, mpo):
    count = lax.axis_size("chan")
    me = lax.axis_index("chan")
    width = current.shape[0]
    held = [current] + [shifted(current, "chan", k) for k in range(1, count)]
    rows = [(me - k) % count for k in range(count)]
    order = jnp.concatenate([jnp.arange(width) + r * width for r in rows])
    return jnp.concatenate(held, axis=0), jnp.take(mpo, order, axis=0)


def advance_line(current, ket, bra, mpo, live_mask, sector, held, pieces, finish):
    gathered, mpo = chan_gathered(current, mpo)
    f32 = jnp.float32
    one = jnp.ones((), f32)
    zero = jnp.zeros((), f32)
    order = jnp.asarray(list(zip(SLOT_A, SLOT_B, LAST_P, (0,) * 4)), jnp.int32)[sector]
    ket = jnp.take(ket, order, axis=0)
    bra = jnp.take(bra, order, axis=0)
    mpo = jnp.take(mpo, order, axis=2)
    slot_a = term(gathered, ket[0], bra[0], mpo[:, :, 0])
    held, slot_a = lax.optimization_barrier((held, slot_a))
    got_right = lax.ppermute(slot_a, "sector", RIGHT)
    middle_left = lax.ppermute(slot_a, "sector", ((3, 1),))
    slot_b = term(gathered, ket[1], bra[1], mpo[:, :, 1])
    got_left = lax.ppermute(slot_b, "sector", LEFT)
    middle_right = lax.ppermute(slot_b, "sector", ((0, 2),))
    third = term(gathered, ket[2], bra[2], mpo[:, :, 2])
    got = (got_right, got_left, middle_right, middle_left, third)
    got_right, got_left, middle_right, middle_left, third = lax.optimization_barrier(got)
    got_middle = middle_right + middle_left
    keep_right = jnp.where(sector == 1, zero, one)
    keep_left = jnp.where(sector == 2, zero, one)
    send = third.astype(f32) + (1 - keep_right) * got_right.astype(f32)
    send = send + (1 - keep_left) * got_left.astype(f32)
    send = send.astype(jnp.bfloat16)
    own = term(gathered, ket[3], bra[3], mpo[:, :, 3])
    total = own.astype(f32) + keep_right * got_right.astype(f32)
    total = total + keep_left * got_left.astype(f32) + got_middle.astype(f32)
    width = send.shape[0]
    bounds = [width * k // pieces for k in range(pieces + 1)]
    results = []
    piece = None
    for low, high in zip(bounds[:-1], bounds[1:]):
        if results:
            piece, send = lax.optimization_barrier((piece, send))
            results[-1] = finish(piece)
        got_last = lax.ppermute(send[low:high], "sector", LAST)
        if results:
            results[-1], got_last = lax.optimization_barrier((results[-1], got_last))
        piece = total[low:high] + got_last.astype(f32)
        piece = (piece * live_mask[None]).astype(jnp.bfloat16)
        results.append(None)
    results[-1] = finish(piece)
    return results, held


def advance_direct(current, ket, bra, mpo, live_mask):
    stride = lax.axis_size("sector") // 2
    gathered, mpo = chan_gathered(current, mpo)
    f32 = jnp.float32
    total = term(gathered, ket[0], bra[0], mpo[:, :, 0]).astype(f32)
    for p, steps in ((1, 1), (2, stride), (3, stride + 1)):
        part = term(gathered, ket[p], bra[p], mpo[:, :, p])
        total = total + shifted(part, "sector", steps).astype(f32)
    return (total * live_mask[None]).astype(jnp.bfloat16)


def shards(environment, ket_tensor, bra_tensor, mpo_tensor, block_length):
    width = environment.shape[-1]
    index = jnp.arange(width, dtype=jnp.int32)
    alive = index < block_length[0]
    live_both = alive[:, None] & alive[None, :]
    live_mask = live_both.astype(jnp.float32)
    sector = lax.axis_index("sector")
    line = lax.axis_size("sector") == 4
    tensors = [(ket_tensor[0, 0], bra_tensor[0, 0], mpo_tensor[0])]
    for _ in range(1, STEPS):
        ket, bra, mpo = tensors[-1]
        tensors.append(tuple(shifted(t, "site", -1) for t in (ket, bra, mpo)))
    current = jnp.where(live_both, environment[0, :, 0], jnp.zeros((), jnp.bfloat16))
    def onward(part):
        return shifted(part[None, :, None], "site", STEPS)

    for step in range(STEPS):
        ket, bra, mpo = tensors[step]
        last = step == STEPS - 1
        if line:
            parts, tensors[step + 1 :] = advance_line(
                current, ket, bra, mpo, live_mask, sector, tensors[step + 1 :],
                2 if last else 1, onward if last else (lambda part: part),
            )
        else:
            parts = [advance_direct(current, ket, bra, mpo, live_mask)]
            parts = [onward(parts[0])] if last else parts
        if not last:
            current = jnp.concatenate(parts, axis=0)
    return jnp.concatenate(parts, axis=1)


def solution(mesh):
    return jax.shard_map(
        shards,
        mesh=mesh,
        in_specs=(
            P("site", "chan", "sector", None, None),
            P("site", "sector", None, None, None),
            P("site", "sector", None, None, None),
            P("site", None, "chan", None),
            P("sector"),
        ),
        out_specs=P("site", "chan", "sector", None, None),
        check_vma=False,
    )
```

```python
import jax
import jax.numpy as jnp
from jax import lax
from jax.sharding import PartitionSpec as P

STEPS = 2

SLOT_A = (3, 1, 1, 2)
SLOT_B = (2, 3, 3, 1)
LAST_P = (1, 2, 2, 3)
RIGHT = ((0, 1), (1, 2), (2, 3))
LEFT = ((3, 2), (2, 1), (1, 0))
LAST = ((0, 1), (1, 3), (3, 2), (2, 0))


def shifted(value, axis, steps):
    count = lax.axis_size(axis)
    pairs = [(source, (source + steps) % count) for source in range(count)]
    return lax.ppermute(value, axis, pairs)


def term(gathered, ket_p, bra_p, mpo_p):
    mixed = jnp.einsum(
        "wv,wba->vba", mpo_p, gathered, preferred_element_type=jnp.float32
    ).astype(jnp.bfloat16)
    rotated = jnp.einsum(
        "vba,ac->vbc", mixed, ket_p, preferred_element_type=jnp.float32
    ).astype(jnp.bfloat16)
    return jnp.einsum(
        "bd,vbc->vdc", bra_p, rotated, preferred_element_type=jnp.float32
    ).astype(jnp.bfloat16)


def chan_gathered(current, mpo):
    count = lax.axis_size("chan")
    me = lax.axis_index("chan")
    width = current.shape[0]
    held = [current] + [shifted(current, "chan", k) for k in range(1, count)]
    rows = [(me - k) % count for k in range(count)]
    order = jnp.concatenate([jnp.arange(width) + r * width for r in rows])
    return jnp.concatenate(held, axis=0), jnp.take(mpo, order, axis=0)


def advance_line(current, ket, bra, mpo, live_mask, sector, held, pieces, finish):
    gathered, mpo = chan_gathered(current, mpo)
    f32 = jnp.float32
    one = jnp.ones((), f32)
    zero = jnp.zeros((), f32)
    order = jnp.asarray(list(zip(SLOT_A, SLOT_B, LAST_P, (0,) * 4)), jnp.int32)[sector]
    ket = jnp.take(ket, order, axis=0)
    bra = jnp.take(bra, order, axis=0)
    mpo = jnp.take(mpo, order, axis=2)
    slot_a = term(gathered, ket[0], bra[0], mpo[:, :, 0])
    held, slot_a = lax.optimization_barrier((held, slot_a))
    got_right = lax.ppermute(slot_a, "sector", RIGHT)
    middle_left = lax.ppermute(slot_a, "sector", ((3, 1),))
    slot_b = term(gathered, ket[1], bra[1], mpo[:, :, 1])
    got_left = lax.ppermute(slot_b, "sector", LEFT)
    middle_right = lax.ppermute(slot_b, "sector", ((0, 2),))
    third = term(gathered, ket[2], bra[2], mpo[:, :, 2])
    got = (got_right, got_left, third)
    got_right, got_left, third = lax.optimization_barrier(got)
    got_middle = middle_right + middle_left
    keep_right = jnp.where(sector == 1, zero, one)
    keep_left = jnp.where(sector == 2, zero, one)
    send = third.astype(f32) + (1 - keep_right) * got_right.astype(f32)
    send = send + (1 - keep_left) * got_left.astype(f32)
    send = send.astype(jnp.bfloat16)
    own = term(gathered, ket[3], bra[3], mpo[:, :, 3])
    total = own.astype(f32) + keep_right * got_right.astype(f32)
    total = total + keep_left * got_left.astype(f32) + got_middle.astype(f32)
    width = send.shape[0]
    bounds = [width * k // pieces for k in range(pieces + 1)]
    results = []
    piece = None
    for low, high in zip(bounds[:-1], bounds[1:]):
        if results:
            piece, send = lax.optimization_barrier((piece, send))
            results[-1] = finish(piece)
        got_last = lax.ppermute(send[low:high], "sector", LAST)
        if results:
            results[-1], got_last = lax.optimization_barrier((results[-1], got_last))
        piece = total[low:high] + got_last.astype(f32)
        piece = (piece * live_mask[None]).astype(jnp.bfloat16)
        results.append(None)
    results[-1] = finish(piece)
    return results, held


def advance_direct(current, ket, bra, mpo, live_mask):
    stride = lax.axis_size("sector") // 2
    gathered, mpo = chan_gathered(current, mpo)
    f32 = jnp.float32
    total = term(gathered, ket[0], bra[0], mpo[:, :, 0]).astype(f32)
    for p, steps in ((1, 1), (2, stride), (3, stride + 1)):
        part = term(gathered, ket[p], bra[p], mpo[:, :, p])
        total = total + shifted(part, "sector", steps).astype(f32)
    return (total * live_mask[None]).astype(jnp.bfloat16)


def shards(environment, ket_tensor, bra_tensor, mpo_tensor, block_length):
    width = environment.shape[-1]
    index = jnp.arange(width, dtype=jnp.int32)
    alive = index < block_length[0]
    live_both = alive[:, None] & alive[None, :]
    live_mask = live_both.astype(jnp.float32)
    sector = lax.axis_index("sector")
    line = lax.axis_size("sector") == 4
    tensors = [(ket_tensor[0, 0], bra_tensor[0, 0], mpo_tensor[0])]
    for _ in range(1, STEPS):
        ket, bra, mpo = tensors[-1]
        tensors.append(tuple(shifted(t, "site", -1) for t in (ket, bra, mpo)))
    current = jnp.where(live_both, environment[0, :, 0], jnp.zeros((), jnp.bfloat16))
    def onward(part):
        return shifted(part[None, :, None], "site", STEPS)

    for step in range(STEPS):
        ket, bra, mpo = tensors[step]
        last = step == STEPS - 1
        if line:
            parts, tensors[step + 1 :] = advance_line(
                current, ket, bra, mpo, live_mask, sector, tensors[step + 1 :],
                2 if last else 1, onward if last else (lambda part: part),
            )
        else:
            parts = [advance_direct(current, ket, bra, mpo, live_mask)]
            parts = [onward(parts[0])] if last else parts
        if not last:
            current = jnp.concatenate(parts, axis=0)
    return jnp.concatenate(parts, axis=1)


def solution(mesh):
    return jax.shard_map(
        shards,
        mesh=mesh,
        in_specs=(
            P("site", "chan", "sector", None, None),
            P("site", "sector", None, None, None),
            P("site", "sector", None, None, None),
            P("site", None, "chan", None),
            P("sector"),
        ),
        out_specs=P("site", "chan", "sector", None, None),
        check_vma=False,
    )
```

```python
import jax
import jax.numpy as jnp
from jax import lax
from jax.sharding import PartitionSpec as P

STEPS = 2

SLOT_A = (3, 1, 1, 2)
SLOT_B = (2, 3, 3, 1)
LAST_P = (1, 2, 2, 3)
RIGHT = ((0, 1), (1, 2), (2, 3))
LEFT = ((3, 2), (2, 1), (1, 0))
LAST = ((0, 1), (1, 3), (3, 2), (2, 0))


def shifted(value, axis, steps):
    count = lax.axis_size(axis)
    pairs = [(source, (source + steps) % count) for source in range(count)]
    return lax.ppermute(value, axis, pairs)


def term(gathered, ket_p, bra_p, mpo_p):
    mixed = jnp.einsum(
        "wv,wba->vba", mpo_p, gathered, preferred_element_type=jnp.float32
    ).astype(jnp.bfloat16)
    rotated = jnp.einsum(
        "vba,ac->vbc", mixed, ket_p, preferred_element_type=jnp.float32
    ).astype(jnp.bfloat16)
    return jnp.einsum(
        "bd,vbc->vdc", bra_p, rotated, preferred_element_type=jnp.float32
    ).astype(jnp.bfloat16)


def chan_gathered(current, mpo):
    count = lax.axis_size("chan")
    me = lax.axis_index("chan")
    width = current.shape[0]
    held = [current] + [shifted(current, "chan", k) for k in range(1, count)]
    rows = [(me - k) % count for k in range(count)]
    order = jnp.concatenate([jnp.arange(width) + r * width for r in rows])
    return jnp.concatenate(held, axis=0), jnp.take(mpo, order, axis=0)


def pick(table, sector, ket, bra, mpo):
    p = jnp.asarray(table, jnp.int32)[sector]
    return (
        lax.dynamic_index_in_dim(ket, p, 0, keepdims=False),
        lax.dynamic_index_in_dim(bra, p, 0, keepdims=False),
        lax.dynamic_index_in_dim(mpo, p, 2, keepdims=False),
    )


def advance_line(current, ket, bra, mpo, live_mask, sector, held, pieces, finish):
    gathered, mpo = chan_gathered(current, mpo)
    f32 = jnp.float32
    one = jnp.ones((), f32)
    zero = jnp.zeros((), f32)
    slot_a = term(gathered, *pick(SLOT_A, sector, ket, bra, mpo))
    held, slot_a = lax.optimization_barrier((held, slot_a))
    got_right = lax.ppermute(slot_a, "sector", RIGHT)
    middle_left = lax.ppermute(slot_a, "sector", ((3, 1),))
    slot_b = term(gathered, *pick(SLOT_B, sector, ket, bra, mpo))
    got_left = lax.ppermute(slot_b, "sector", LEFT)
    middle_right = lax.ppermute(slot_b, "sector", ((0, 2),))
    third = term(gathered, *pick(LAST_P, sector, ket, bra, mpo))
    got = (got_right, got_left, middle_right, middle_left, third)
    got_right, got_left, middle_right, middle_left, third = lax.optimization_barrier(got)
    got_middle = middle_right + middle_left
    keep_right = jnp.where(sector == 1, zero, one)
    keep_left = jnp.where(sector == 2, zero, one)
    send = third.astype(f32) + (1 - keep_right) * got_right.astype(f32)
    send = send + (1 - keep_left) * got_left.astype(f32)
    send = send.astype(jnp.bfloat16)
    own = term(gathered, ket[0], bra[0], mpo[:, :, 0])
    total = own.astype(f32) + keep_right * got_right.astype(f32)
    total = total + keep_left * got_left.astype(f32) + got_middle.astype(f32)
    width = send.shape[0]
    bounds = [width * k // pieces for k in range(pieces + 1)]
    results = []
    piece = None
    for low, high in zip(bounds[:-1], bounds[1:]):
        if results:
            piece, send = lax.optimization_barrier((piece, send))
            results[-1] = finish(piece)
        got_last = lax.ppermute(send[low:high], "sector", LAST)
        if results:
            results[-1], got_last = lax.optimization_barrier((results[-1], got_last))
        piece = total[low:high] + got_last.astype(f32)
        piece = (piece * live_mask[None]).astype(jnp.bfloat16)
        results.append(None)
    results[-1] = finish(piece)
    return results, held


def advance_direct(current, ket, bra, mpo, live_mask):
    stride = lax.axis_size("sector") // 2
    gathered, mpo = chan_gathered(current, mpo)
    f32 = jnp.float32
    total = term(gathered, ket[0], bra[0], mpo[:, :, 0]).astype(f32)
    for p, steps in ((1, 1), (2, stride), (3, stride + 1)):
        part = term(gathered, ket[p], bra[p], mpo[:, :, p])
        total = total + shifted(part, "sector", steps).astype(f32)
    return (total * live_mask[None]).astype(jnp.bfloat16)


def shards(environment, ket_tensor, bra_tensor, mpo_tensor, block_length):
    width = environment.shape[-1]
    index = jnp.arange(width, dtype=jnp.int32)
    alive = index < block_length[0]
    live_both = alive[:, None] & alive[None, :]
    live_mask = live_both.astype(jnp.float32)
    sector = lax.axis_index("sector")
    line = lax.axis_size("sector") == 4
    tensors = [(ket_tensor[0, 0], bra_tensor[0, 0], mpo_tensor[0])]
    for _ in range(1, STEPS):
        ket, bra, mpo = tensors[-1]
        tensors.append(tuple(shifted(t, "site", -1) for t in (ket, bra, mpo)))
    current = jnp.where(live_both, environment[0, :, 0], jnp.zeros((), jnp.bfloat16))
    def onward(part):
        return shifted(part[None, :, None], "site", STEPS)

    for step in range(STEPS):
        ket, bra, mpo = tensors[step]
        last = step == STEPS - 1
        if line:
            parts, tensors[step + 1 :] = advance_line(
                current, ket, bra, mpo, live_mask, sector, tensors[step + 1 :],
                3 if last else 1, onward if last else (lambda part: part),
            )
        else:
            parts = [advance_direct(current, ket, bra, mpo, live_mask)]
            parts = [onward(parts[0])] if last else parts
        if not last:
            current = jnp.concatenate(parts, axis=0)
    return jnp.concatenate(parts, axis=1)


def solution(mesh):
    return jax.shard_map(
        shards,
        mesh=mesh,
        in_specs=(
            P("site", "chan", "sector", None, None),
            P("site", "sector", None, None, None),
            P("site", "sector", None, None, None),
            P("site", None, "chan", None),
            P("sector"),
        ),
        out_specs=P("site", "chan", "sector", None, None),
        check_vma=False,
    )
```

```python
import jax
import jax.numpy as jnp
from jax import lax
from jax.sharding import PartitionSpec as P

STEPS = 2

SLOT_A = (3, 1, 1, 2)
SLOT_B = (2, 3, 3, 1)
LAST_P = (1, 2, 2, 3)
RIGHT = ((0, 1), (1, 2), (2, 3))
LEFT = ((3, 2), (2, 1), (1, 0))
LAST = ((0, 1), (1, 3), (3, 2), (2, 0))


def shifted(value, axis, steps):
    count = lax.axis_size(axis)
    pairs = [(source, (source + steps) % count) for source in range(count)]
    return lax.ppermute(value, axis, pairs)


def term(gathered, ket_p, bra_p, mpo_p):
    mixed = jnp.einsum(
        "wv,wba->vba", mpo_p, gathered, preferred_element_type=jnp.float32
    ).astype(jnp.bfloat16)
    rotated = jnp.einsum(
        "vba,ac->vbc", mixed, ket_p, preferred_element_type=jnp.float32
    ).astype(jnp.bfloat16)
    return jnp.einsum(
        "bd,vbc->vdc", bra_p, rotated, preferred_element_type=jnp.float32
    ).astype(jnp.bfloat16)


def chan_gathered(current, mpo):
    count = lax.axis_size("chan")
    me = lax.axis_index("chan")
    width = current.shape[0]
    held = [current] + [shifted(current, "chan", k) for k in range(1, count)]
    rows = [(me - k) % count for k in range(count)]
    order = jnp.concatenate([jnp.arange(width) + r * width for r in rows])
    return jnp.concatenate(held, axis=0), jnp.take(mpo, order, axis=0)


def pick(table, sector, ket, bra, mpo):
    p = jnp.asarray(table, jnp.int32)[sector]
    return (
        lax.dynamic_index_in_dim(ket, p, 0, keepdims=False),
        lax.dynamic_index_in_dim(bra, p, 0, keepdims=False),
        lax.dynamic_index_in_dim(mpo, p, 2, keepdims=False),
    )


def advance_line(current, ket, bra, mpo, live_mask, sector, held, pieces, finish):
    gathered, mpo = chan_gathered(current, mpo)
    f32 = jnp.float32
    one = jnp.ones((), f32)
    zero = jnp.zeros((), f32)
    slot_a = term(gathered, *pick(SLOT_A, sector, ket, bra, mpo))
    held, slot_a = lax.optimization_barrier((held, slot_a))
    got_right = lax.ppermute(slot_a, "sector", RIGHT)
    middle_left = lax.ppermute(slot_a, "sector", ((3, 1),))
    slot_b = term(gathered, *pick(SLOT_B, sector, ket, bra, mpo))
    got_left = lax.ppermute(slot_b, "sector", LEFT)
    middle_right = lax.ppermute(slot_b, "sector", ((0, 2),))
    third = term(gathered, *pick(LAST_P, sector, ket, bra, mpo))
    got = (got_right, got_left, middle_right, middle_left, third)
    got_right, got_left, middle_right, middle_left, third = lax.optimization_barrier(got)
    got_middle = middle_right + middle_left
    keep_right = jnp.where(sector == 1, zero, one)
    keep_left = jnp.where(sector == 2, zero, one)
    send = third.astype(f32) + (1 - keep_right) * got_right.astype(f32)
    send = send + (1 - keep_left) * got_left.astype(f32)
    send = send.astype(jnp.bfloat16)
    own = term(gathered, ket[0], bra[0], mpo[:, :, 0])
    total = own.astype(f32) + keep_right * got_right.astype(f32)
    total = total + keep_left * got_left.astype(f32) + got_middle.astype(f32)
    width = send.shape[0]
    bounds = [width * k // pieces for k in range(pieces + 1)]
    results = []
    piece = None
    for low, high in zip(bounds[:-1], bounds[1:]):
        if results:
            piece, send = lax.optimization_barrier((piece, send))
            results[-1] = finish(piece)
        got_last = lax.ppermute(send[low:high], "sector", LAST)
        if results:
            results[-1], got_last = lax.optimization_barrier((results[-1], got_last))
        piece = total[low:high] + got_last.astype(f32)
        piece = (piece * live_mask[None]).astype(jnp.bfloat16)
        results.append(None)
    results[-1] = finish(piece)
    return results, held


def advance_direct(current, ket, bra, mpo, live_mask):
    stride = lax.axis_size("sector") // 2
    gathered, mpo = chan_gathered(current, mpo)
    f32 = jnp.float32
    total = term(gathered, ket[0], bra[0], mpo[:, :, 0]).astype(f32)
    for p, steps in ((1, 1), (2, stride), (3, stride + 1)):
        part = term(gathered, ket[p], bra[p], mpo[:, :, p])
        total = total + shifted(part, "sector", steps).astype(f32)
    return (total * live_mask[None]).astype(jnp.bfloat16)


def shards(environment, ket_tensor, bra_tensor, mpo_tensor, block_length):
    width = environment.shape[-1]
    index = jnp.arange(width, dtype=jnp.int32)
    alive = index < block_length[0]
    live_both = alive[:, None] & alive[None, :]
    live_mask = live_both.astype(jnp.float32)
    sector = lax.axis_index("sector")
    line = lax.axis_size("sector") == 4
    tensors = [(ket_tensor[0, 0], bra_tensor[0, 0], mpo_tensor[0])]
    for _ in range(1, STEPS):
        ket, bra, mpo = tensors[-1]
        tensors.append(tuple(shifted(t, "site", -1) for t in (ket, bra, mpo)))
    current = jnp.where(live_both, environment[0, :, 0], jnp.zeros((), jnp.bfloat16))
    def onward(part):
        return shifted(part[None, :, None], "site", STEPS)

    for step in range(STEPS):
        ket, bra, mpo = tensors[step]
        last = step == STEPS - 1
        if line:
            parts, tensors[step + 1 :] = advance_line(
                current, ket, bra, mpo, live_mask, sector, tensors[step + 1 :],
                5 if last else 1, onward if last else (lambda part: part),
            )
        else:
            parts = [advance_direct(current, ket, bra, mpo, live_mask)]
            parts = [onward(parts[0])] if last else parts
        if not last:
            current = jnp.concatenate(parts, axis=0)
    return jnp.concatenate(parts, axis=1)


def solution(mesh):
    return jax.shard_map(
        shards,
        mesh=mesh,
        in_specs=(
            P("site", "chan", "sector", None, None),
            P("site", "sector", None, None, None),
            P("site", "sector", None, None, None),
            P("site", None, "chan", None),
            P("sector"),
        ),
        out_specs=P("site", "chan", "sector", None, None),
        check_vma=False,
    )
```

```python
import jax
import jax.numpy as jnp
from jax import lax
from jax.sharding import PartitionSpec as P

STEPS = 2

SLOT_A = (3, 1, 1, 2)
SLOT_B = (2, 3, 3, 1)
LAST_P = (1, 2, 2, 3)
RIGHT = ((0, 1), (1, 2), (2, 3))
LEFT = ((3, 2), (2, 1), (1, 0))
LAST = ((0, 1), (1, 3), (3, 2), (2, 0))


def shifted(value, axis, steps):
    count = lax.axis_size(axis)
    pairs = [(source, (source + steps) % count) for source in range(count)]
    return lax.ppermute(value, axis, pairs)


def term(gathered, ket_p, bra_p, mpo_p):
    mixed = jnp.einsum(
        "wv,wba->vba", mpo_p, gathered, preferred_element_type=jnp.float32
    ).astype(jnp.bfloat16)
    rotated = jnp.einsum(
        "vba,ac->vbc", mixed, ket_p, preferred_element_type=jnp.float32
    ).astype(jnp.bfloat16)
    return jnp.einsum(
        "bd,vbc->vdc", bra_p, rotated, preferred_element_type=jnp.float32
    ).astype(jnp.bfloat16)


def chan_copies(piece):
    return [piece] + [shifted(piece, "chan", k) for k in range(1, lax.axis_size("chan"))]


def chan_gathered(pieces, mpo):
    count = lax.axis_size("chan")
    me = lax.axis_index("chan")
    held = [jnp.concatenate([p[k] for p in pieces], axis=0) for k in range(count)]
    width = held[0].shape[0]
    rows = [(me - k) % count for k in range(count)]
    order = jnp.concatenate([jnp.arange(width) + r * width for r in rows])
    return jnp.concatenate(held, axis=0), jnp.take(mpo, order, axis=0)


def pick(table, sector, ket, bra, mpo):
    p = jnp.asarray(table, jnp.int32)[sector]
    return (
        lax.dynamic_index_in_dim(ket, p, 0, keepdims=False),
        lax.dynamic_index_in_dim(bra, p, 0, keepdims=False),
        lax.dynamic_index_in_dim(mpo, p, 2, keepdims=False),
    )


def advance_line(current, ket, bra, mpo, live_mask, sector, held, pieces, finish):
    gathered, mpo = chan_gathered(current, mpo)
    f32 = jnp.float32
    one = jnp.ones((), f32)
    zero = jnp.zeros((), f32)
    slot_a = term(gathered, *pick(SLOT_A, sector, ket, bra, mpo))
    held, slot_a = lax.optimization_barrier((held, slot_a))
    got_right = lax.ppermute(slot_a, "sector", RIGHT)
    middle_left = lax.ppermute(slot_a, "sector", ((3, 1),))
    slot_b = term(gathered, *pick(SLOT_B, sector, ket, bra, mpo))
    got_left = lax.ppermute(slot_b, "sector", LEFT)
    middle_right = lax.ppermute(slot_b, "sector", ((0, 2),))
    third = term(gathered, *pick(LAST_P, sector, ket, bra, mpo))
    got = (got_right, got_left, middle_right, middle_left, third)
    got_right, got_left, middle_right, middle_left, third = lax.optimization_barrier(got)
    got_middle = middle_right + middle_left
    keep_right = jnp.where(sector == 1, zero, one)
    keep_left = jnp.where(sector == 2, zero, one)
    send = third.astype(f32) + (1 - keep_right) * got_right.astype(f32)
    send = send + (1 - keep_left) * got_left.astype(f32)
    send = send.astype(jnp.bfloat16)
    own = term(gathered, ket[0], bra[0], mpo[:, :, 0])
    total = own.astype(f32) + keep_right * got_right.astype(f32)
    total = total + keep_left * got_left.astype(f32) + got_middle.astype(f32)
    width = send.shape[0]
    bounds = [width * k // pieces for k in range(pieces + 1)]
    results = []
    piece = None
    for low, high in zip(bounds[:-1], bounds[1:]):
        if results:
            piece, send = lax.optimization_barrier((piece, send))
            results[-1] = finish(piece)
        got_last = lax.ppermute(send[low:high], "sector", LAST)
        if results:
            results[-1], got_last = lax.optimization_barrier((results[-1], got_last))
        piece = total[low:high] + got_last.astype(f32)
        piece = (piece * live_mask[None]).astype(jnp.bfloat16)
        results.append(None)
    results[-1] = finish(piece)
    return results, held


def advance_direct(current, ket, bra, mpo, live_mask):
    stride = lax.axis_size("sector") // 2
    gathered, mpo = chan_gathered(current, mpo)
    f32 = jnp.float32
    total = term(gathered, ket[0], bra[0], mpo[:, :, 0]).astype(f32)
    for p, steps in ((1, 1), (2, stride), (3, stride + 1)):
        part = term(gathered, ket[p], bra[p], mpo[:, :, p])
        total = total + shifted(part, "sector", steps).astype(f32)
    return (total * live_mask[None]).astype(jnp.bfloat16)


def shards(environment, ket_tensor, bra_tensor, mpo_tensor, block_length):
    width = environment.shape[-1]
    index = jnp.arange(width, dtype=jnp.int32)
    alive = index < block_length[0]
    live_both = alive[:, None] & alive[None, :]
    live_mask = live_both.astype(jnp.float32)
    sector = lax.axis_index("sector")
    line = lax.axis_size("sector") == 4
    tensors = [(ket_tensor[0, 0], bra_tensor[0, 0], mpo_tensor[0])]
    for _ in range(1, STEPS):
        ket, bra, mpo = tensors[-1]
        tensors.append(tuple(shifted(t, "site", -1) for t in (ket, bra, mpo)))
    current = jnp.where(live_both, environment[0, :, 0], jnp.zeros((), jnp.bfloat16))
    def onward(part):
        return shifted(part[None, :, None], "site", STEPS)

    pieces = [chan_copies(current)]
    current = None
    for step in range(STEPS):
        ket, bra, mpo = tensors[step]
        last = step == STEPS - 1
        if line:
            parts, tensors[step + 1 :] = advance_line(
                pieces, ket, bra, mpo, live_mask, sector, tensors[step + 1 :],
                3 if last else 2, onward if last else chan_copies,
            )
        else:
            parts = [advance_direct(pieces, ket, bra, mpo, live_mask)]
            current = parts[0]
            parts = [onward(current)] if last else [chan_copies(current)]
        pieces = parts
    return jnp.concatenate(pieces, axis=1)


def solution(mesh):
    return jax.shard_map(
        shards,
        mesh=mesh,
        in_specs=(
            P("site", "chan", "sector", None, None),
            P("site", "sector", None, None, None),
            P("site", "sector", None, None, None),
            P("site", None, "chan", None),
            P("sector"),
        ),
        out_specs=P("site", "chan", "sector", None, None),
        check_vma=False,
    )
```

```python
import jax
import jax.numpy as jnp
from jax import lax
from jax.sharding import PartitionSpec as P

STEPS = 2

SLOT_A = (3, 1, 1, 2)
SLOT_B = (2, 3, 3, 1)
LAST_P = (1, 2, 2, 3)
RIGHT = ((0, 1), (1, 2), (2, 3))
LEFT = ((3, 2), (2, 1), (1, 0))
LAST = ((0, 1), (1, 3), (3, 2), (2, 0))


def shifted(value, axis, steps):
    count = lax.axis_size(axis)
    pairs = [(source, (source + steps) % count) for source in range(count)]
    return lax.ppermute(value, axis, pairs)


def term(gathered, ket_p, bra_p, mpo_p):
    mixed = jnp.einsum(
        "wv,wba->vba", mpo_p, gathered, preferred_element_type=jnp.float32
    ).astype(jnp.bfloat16)
    rotated = jnp.einsum(
        "vba,ac->vbc", mixed, ket_p, preferred_element_type=jnp.float32
    ).astype(jnp.bfloat16)
    return jnp.einsum(
        "bd,vbc->vdc", bra_p, rotated, preferred_element_type=jnp.float32
    ).astype(jnp.bfloat16)


def chan_copies(piece):
    return [piece] + [shifted(piece, "chan", k) for k in range(1, lax.axis_size("chan"))]


def chan_gathered(pieces, mpo):
    count = lax.axis_size("chan")
    me = lax.axis_index("chan")
    held = [jnp.concatenate([p[k] for p in pieces], axis=0) for k in range(count)]
    width = held[0].shape[0]
    rows = [(me - k) % count for k in range(count)]
    order = jnp.concatenate([jnp.arange(width) + r * width for r in rows])
    return jnp.concatenate(held, axis=0), jnp.take(mpo, order, axis=0)


def pick(table, sector, ket, bra, mpo):
    p = jnp.asarray(table, jnp.int32)[sector]
    return (
        lax.dynamic_index_in_dim(ket, p, 0, keepdims=False),
        lax.dynamic_index_in_dim(bra, p, 0, keepdims=False),
        lax.dynamic_index_in_dim(mpo, p, 2, keepdims=False),
    )


def advance_line(current, ket, bra, mpo, live_mask, sector, held, pieces, finish):
    gathered, mpo = chan_gathered(current, mpo)
    f32 = jnp.float32
    one = jnp.ones((), f32)
    zero = jnp.zeros((), f32)
    slot_a = term(gathered, *pick(SLOT_A, sector, ket, bra, mpo))
    held, slot_a = lax.optimization_barrier((held, slot_a))
    got_right = lax.ppermute(slot_a, "sector", RIGHT)
    middle_left = lax.ppermute(slot_a, "sector", ((3, 1),))
    slot_b = term(gathered, *pick(SLOT_B, sector, ket, bra, mpo))
    got_left = lax.ppermute(slot_b, "sector", LEFT)
    middle_right = lax.ppermute(slot_b, "sector", ((0, 2),))
    third = term(gathered, *pick(LAST_P, sector, ket, bra, mpo))
    got = (got_right, got_left, middle_right, middle_left, third)
    got_right, got_left, middle_right, middle_left, third = lax.optimization_barrier(got)
    got_middle = middle_right + middle_left
    keep_right = jnp.where(sector == 1, zero, one)
    keep_left = jnp.where(sector == 2, zero, one)
    send = third.astype(f32) + (1 - keep_right) * got_right.astype(f32)
    send = send + (1 - keep_left) * got_left.astype(f32)
    send = send.astype(jnp.bfloat16)
    own = term(gathered, ket[0], bra[0], mpo[:, :, 0])
    total = own.astype(f32) + keep_right * got_right.astype(f32)
    total = total + keep_left * got_left.astype(f32) + got_middle.astype(f32)
    width = send.shape[0]
    bounds = [width * k // pieces for k in range(pieces + 1)]
    results = []
    piece = None
    for low, high in zip(bounds[:-1], bounds[1:]):
        if results:
            piece, send = lax.optimization_barrier((piece, send))
            results[-1] = finish(piece)
        got_last = lax.ppermute(send[low:high], "sector", LAST)
        if results:
            results[-1], got_last = lax.optimization_barrier((results[-1], got_last))
        piece = total[low:high] + got_last.astype(f32)
        piece = (piece * live_mask[None]).astype(jnp.bfloat16)
        results.append(None)
    results[-1] = finish(piece)
    return results, held


def advance_direct(current, ket, bra, mpo, live_mask):
    stride = lax.axis_size("sector") // 2
    gathered, mpo = chan_gathered(current, mpo)
    f32 = jnp.float32
    total = term(gathered, ket[0], bra[0], mpo[:, :, 0]).astype(f32)
    for p, steps in ((1, 1), (2, stride), (3, stride + 1)):
        part = term(gathered, ket[p], bra[p], mpo[:, :, p])
        total = total + shifted(part, "sector", steps).astype(f32)
    return (total * live_mask[None]).astype(jnp.bfloat16)


def shards(environment, ket_tensor, bra_tensor, mpo_tensor, block_length):
    width = environment.shape[-1]
    index = jnp.arange(width, dtype=jnp.int32)
    alive = index < block_length[0]
    live_both = alive[:, None] & alive[None, :]
    live_mask = live_both.astype(jnp.float32)
    sector = lax.axis_index("sector")
    line = lax.axis_size("sector") == 4
    tensors = [(ket_tensor[0, 0], bra_tensor[0, 0], mpo_tensor[0])]
    for _ in range(1, STEPS):
        ket, bra, mpo = tensors[-1]
        tensors.append(tuple(shifted(t, "site", -1) for t in (ket, bra, mpo)))
    current = jnp.where(live_both, environment[0, :, 0], jnp.zeros((), jnp.bfloat16))
    def onward(part):
        return shifted(part[None, :, None], "site", STEPS)

    pieces = [chan_copies(current)]
    current = None
    for step in range(STEPS):
        ket, bra, mpo = tensors[step]
        last = step == STEPS - 1
        if line:
            parts, tensors[step + 1 :] = advance_line(
                pieces, ket, bra, mpo, live_mask, sector, tensors[step + 1 :],
                3 if last else 3, onward if last else chan_copies,
            )
        else:
            parts = [advance_direct(pieces, ket, bra, mpo, live_mask)]
            current = parts[0]
            parts = [onward(current)] if last else [chan_copies(current)]
        pieces = parts
    return jnp.concatenate(pieces, axis=1)


def solution(mesh):
    return jax.shard_map(
        shards,
        mesh=mesh,
        in_specs=(
            P("site", "chan", "sector", None, None),
            P("site", "sector", None, None, None),
            P("site", "sector", None, None, None),
            P("site", None, "chan", None),
            P("sector"),
        ),
        out_specs=P("site", "chan", "sector", None, None),
        check_vma=False,
    )
```

```python
import jax
import jax.numpy as jnp
from jax import lax
from jax.sharding import PartitionSpec as P

STEPS = 2

SLOT_A = (3, 1, 1, 2)
SLOT_B = (2, 3, 3, 1)
LAST_P = (1, 2, 2, 3)
RIGHT = ((0, 1), (1, 2), (2, 3))
LEFT = ((3, 2), (2, 1), (1, 0))
LAST = ((0, 1), (1, 3), (3, 2), (2, 0))


def shifted(value, axis, steps):
    count = lax.axis_size(axis)
    pairs = [(source, (source + steps) % count) for source in range(count)]
    return lax.ppermute(value, axis, pairs)


def term(gathered, ket_p, bra_p, mpo_p):
    mixed = jnp.einsum(
        "wv,wba->vba", mpo_p, gathered, preferred_element_type=jnp.float32
    ).astype(jnp.bfloat16)
    rotated = jnp.einsum(
        "vba,ac->vbc", mixed, ket_p, preferred_element_type=jnp.float32
    ).astype(jnp.bfloat16)
    return jnp.einsum(
        "bd,vbc->vdc", bra_p, rotated, preferred_element_type=jnp.float32
    ).astype(jnp.bfloat16)


def chan_copies(piece):
    return [piece] + [shifted(piece, "chan", k) for k in range(1, lax.axis_size("chan"))]


def chan_gathered(pieces, mpo):
    count = lax.axis_size("chan")
    me = lax.axis_index("chan")
    held = [jnp.concatenate([p[k] for p in pieces], axis=0) for k in range(count)]
    width = held[0].shape[0]
    rows = [(me - k) % count for k in range(count)]
    order = jnp.concatenate([jnp.arange(width) + r * width for r in rows])
    return jnp.concatenate(held, axis=0), jnp.take(mpo, order, axis=0)


def pick(table, sector, ket, bra, mpo):
    p = jnp.asarray(table, jnp.int32)[sector]
    return (
        lax.dynamic_index_in_dim(ket, p, 0, keepdims=False),
        lax.dynamic_index_in_dim(bra, p, 0, keepdims=False),
        lax.dynamic_index_in_dim(mpo, p, 2, keepdims=False),
    )


def advance_line(current, ket, bra, mpo, live_mask, sector, held, pieces, finish):
    gathered, mpo = chan_gathered(current, mpo)
    f32 = jnp.float32
    one = jnp.ones((), f32)
    zero = jnp.zeros((), f32)
    slot_a = term(gathered, *pick(SLOT_A, sector, ket, bra, mpo))
    held, slot_a = lax.optimization_barrier((held, slot_a))
    got_right = lax.ppermute(slot_a, "sector", RIGHT)
    middle_left = lax.ppermute(slot_a, "sector", ((3, 1),))
    slot_b = term(gathered, *pick(SLOT_B, sector, ket, bra, mpo))
    got_left = lax.ppermute(slot_b, "sector", LEFT)
    middle_right = lax.ppermute(slot_b, "sector", ((0, 2),))
    third = term(gathered, *pick(LAST_P, sector, ket, bra, mpo))
    got = (got_right, got_left, middle_right, middle_left, third)
    got_right, got_left, middle_right, middle_left, third = lax.optimization_barrier(got)
    got_middle = middle_right + middle_left
    keep_right = jnp.where(sector == 1, zero, one)
    keep_left = jnp.where(sector == 2, zero, one)
    send = third.astype(f32) + (1 - keep_right) * got_right.astype(f32)
    send = send + (1 - keep_left) * got_left.astype(f32)
    send = send.astype(jnp.bfloat16)
    own = term(gathered, ket[0], bra[0], mpo[:, :, 0])
    total = own.astype(f32) + keep_right * got_right.astype(f32)
    total = total + keep_left * got_left.astype(f32) + got_middle.astype(f32)
    width = send.shape[0]
    bounds = [width * k // pieces for k in range(pieces + 1)]
    results = []
    piece = None
    for low, high in zip(bounds[:-1], bounds[1:]):
        if results:
            piece, send = lax.optimization_barrier((piece, send))
            results[-1] = finish(piece)
        got_last = lax.ppermute(send[low:high], "sector", LAST)
        if results:
            results[-1], got_last = lax.optimization_barrier((results[-1], got_last))
        piece = total[low:high] + got_last.astype(f32)
        piece = (piece * live_mask[None]).astype(jnp.bfloat16)
        results.append(None)
    results[-1] = finish(piece)
    return results, held


def advance_direct(current, ket, bra, mpo, live_mask):
    stride = lax.axis_size("sector") // 2
    gathered, mpo = chan_gathered(current, mpo)
    f32 = jnp.float32
    total = term(gathered, ket[0], bra[0], mpo[:, :, 0]).astype(f32)
    for p, steps in ((1, 1), (2, stride), (3, stride + 1)):
        part = term(gathered, ket[p], bra[p], mpo[:, :, p])
        total = total + shifted(part, "sector", steps).astype(f32)
    return (total * live_mask[None]).astype(jnp.bfloat16)


def shards(environment, ket_tensor, bra_tensor, mpo_tensor, block_length):
    width = environment.shape[-1]
    index = jnp.arange(width, dtype=jnp.int32)
    alive = index < block_length[0]
    live_both = alive[:, None] & alive[None, :]
    live_mask = live_both.astype(jnp.float32)
    sector = lax.axis_index("sector")
    line = lax.axis_size("sector") == 4
    tensors = [(ket_tensor[0, 0], bra_tensor[0, 0], mpo_tensor[0])]
    for _ in range(1, STEPS):
        ket, bra, mpo = tensors[-1]
        tensors.append(tuple(shifted(t, "site", -1) for t in (ket, bra, mpo)))
    current = jnp.where(live_both, environment[0, :, 0], jnp.zeros((), jnp.bfloat16))
    def onward(part):
        return shifted(part[None, :, None], "site", STEPS)

    pieces = [chan_copies(current)]
    current = None
    for step in range(STEPS):
        ket, bra, mpo = tensors[step]
        last = step == STEPS - 1
        if line:
            parts, tensors[step + 1 :] = advance_line(
                pieces, ket, bra, mpo, live_mask, sector, tensors[step + 1 :],
                4 if last else 2, onward if last else chan_copies,
            )
        else:
            parts = [advance_direct(pieces, ket, bra, mpo, live_mask)]
            current = parts[0]
            parts = [onward(current)] if last else [chan_copies(current)]
        pieces = parts
    return jnp.concatenate(pieces, axis=1)


def solution(mesh):
    return jax.shard_map(
        shards,
        mesh=mesh,
        in_specs=(
            P("site", "chan", "sector", None, None),
            P("site", "sector", None, None, None),
            P("site", "sector", None, None, None),
            P("site", None, "chan", None),
            P("sector"),
        ),
        out_specs=P("site", "chan", "sector", None, None),
        check_vma=False,
    )
```

```python
import jax
import jax.numpy as jnp
from jax import lax
from jax.sharding import PartitionSpec as P

STEPS = 2

SLOT_A = (3, 1, 1, 2)
SLOT_B = (2, 3, 3, 1)
LAST_P = (1, 2, 2, 3)
RIGHT = ((0, 1), (1, 2), (2, 3))
LEFT = ((3, 2), (2, 1), (1, 0))
LAST = ((0, 1), (1, 3), (3, 2), (2, 0))


def shifted(value, axis, steps):
    count = lax.axis_size(axis)
    pairs = [(source, (source + steps) % count) for source in range(count)]
    return lax.ppermute(value, axis, pairs)


def term(gathered, ket_p, bra_p, mpo_p):
    mixed = jnp.einsum(
        "wv,wba->vba", mpo_p, gathered, preferred_element_type=jnp.float32
    ).astype(jnp.bfloat16)
    rotated = jnp.einsum(
        "vba,ac->vbc", mixed, ket_p, preferred_element_type=jnp.float32
    ).astype(jnp.bfloat16)
    return jnp.einsum(
        "bd,vbc->vdc", bra_p, rotated, preferred_element_type=jnp.float32
    ).astype(jnp.bfloat16)


def chan_copies(piece):
    return [piece] + [shifted(piece, "chan", k) for k in range(1, lax.axis_size("chan"))]


def chan_gathered(pieces, mpo):
    count = lax.axis_size("chan")
    me = lax.axis_index("chan")
    held = [jnp.concatenate([p[k] for p in pieces], axis=0) for k in range(count)]
    width = held[0].shape[0]
    rows = [(me - k) % count for k in range(count)]
    order = jnp.concatenate([jnp.arange(width) + r * width for r in rows])
    return jnp.concatenate(held, axis=0), jnp.take(mpo, order, axis=0)


def pick(table, sector, ket, bra, mpo):
    p = jnp.asarray(table, jnp.int32)[sector]
    return (
        lax.dynamic_index_in_dim(ket, p, 0, keepdims=False),
        lax.dynamic_index_in_dim(bra, p, 0, keepdims=False),
        lax.dynamic_index_in_dim(mpo, p, 2, keepdims=False),
    )


def advance_line(current, ket, bra, mpo, live_mask, sector, held, pieces, finish):
    gathered, mpo = chan_gathered(current, mpo)
    f32 = jnp.float32
    one = jnp.ones((), f32)
    zero = jnp.zeros((), f32)
    slot_a = term(gathered, *pick(SLOT_A, sector, ket, bra, mpo))
    held, slot_a = lax.optimization_barrier((held, slot_a))
    got_right = lax.ppermute(slot_a, "sector", RIGHT)
    middle_left = lax.ppermute(slot_a, "sector", ((3, 1),))
    slot_b = term(gathered, *pick(SLOT_B, sector, ket, bra, mpo))
    got_left = lax.ppermute(slot_b, "sector", LEFT)
    middle_right = lax.ppermute(slot_b, "sector", ((0, 2),))
    third = term(gathered, *pick(LAST_P, sector, ket, bra, mpo))
    got = (got_right, got_left, middle_right, middle_left, third)
    got_right, got_left, middle_right, middle_left, third = lax.optimization_barrier(got)
    got_middle = middle_right + middle_left
    keep_right = jnp.where(sector == 1, zero, one)
    keep_left = jnp.where(sector == 2, zero, one)
    own = term(gathered, ket[0], bra[0], mpo[:, :, 0])
    total = own.astype(f32) + keep_right * got_right.astype(f32)
    total = total + keep_left * got_left.astype(f32) + got_middle.astype(f32)
    width = third.shape[0]
    bounds = [width * k // pieces for k in range(pieces + 1)]
    results = []
    piece = None
    for low, high in zip(bounds[:-1], bounds[1:]):
        send = third[low:high].astype(f32)
        send = send + (1 - keep_right) * got_right[low:high].astype(f32)
        send = send + (1 - keep_left) * got_left[low:high].astype(f32)
        send = send.astype(jnp.bfloat16)
        if results:
            piece, send = lax.optimization_barrier((piece, send))
            results[-1] = finish(piece)
        got_last = lax.ppermute(send, "sector", LAST)
        if results:
            results[-1], got_last = lax.optimization_barrier((results[-1], got_last))
        piece = total[low:high] + got_last.astype(f32)
        piece = (piece * live_mask[None]).astype(jnp.bfloat16)
        results.append(None)
    results[-1] = finish(piece)
    return results, held


def advance_direct(current, ket, bra, mpo, live_mask):
    stride = lax.axis_size("sector") // 2
    gathered, mpo = chan_gathered(current, mpo)
    f32 = jnp.float32
    total = term(gathered, ket[0], bra[0], mpo[:, :, 0]).astype(f32)
    for p, steps in ((1, 1), (2, stride), (3, stride + 1)):
        part = term(gathered, ket[p], bra[p], mpo[:, :, p])
        total = total + shifted(part, "sector", steps).astype(f32)
    return (total * live_mask[None]).astype(jnp.bfloat16)


def shards(environment, ket_tensor, bra_tensor, mpo_tensor, block_length):
    width = environment.shape[-1]
    index = jnp.arange(width, dtype=jnp.int32)
    alive = index < block_length[0]
    live_both = alive[:, None] & alive[None, :]
    live_mask = live_both.astype(jnp.float32)
    sector = lax.axis_index("sector")
    line = lax.axis_size("sector") == 4
    tensors = [(ket_tensor[0, 0], bra_tensor[0, 0], mpo_tensor[0])]
    for _ in range(1, STEPS):
        ket, bra, mpo = tensors[-1]
        tensors.append(tuple(shifted(t, "site", -1) for t in (ket, bra, mpo)))
    current = jnp.where(live_both, environment[0, :, 0], jnp.zeros((), jnp.bfloat16))
    def onward(part):
        return shifted(part[None, :, None], "site", STEPS)

    pieces = [chan_copies(current)]
    current = None
    for step in range(STEPS):
        ket, bra, mpo = tensors[step]
        last = step == STEPS - 1
        if line:
            parts, tensors[step + 1 :] = advance_line(
                pieces, ket, bra, mpo, live_mask, sector, tensors[step + 1 :],
                3 if last else 2, onward if last else chan_copies,
            )
        else:
            parts = [advance_direct(pieces, ket, bra, mpo, live_mask)]
            current = parts[0]
            parts = [onward(current)] if last else [chan_copies(current)]
        pieces = parts
    return jnp.concatenate(pieces, axis=1)


def solution(mesh):
    return jax.shard_map(
        shards,
        mesh=mesh,
        in_specs=(
            P("site", "chan", "sector", None, None),
            P("site", "sector", None, None, None),
            P("site", "sector", None, None, None),
            P("site", None, "chan", None),
            P("sector"),
        ),
        out_specs=P("site", "chan", "sector", None, None),
        check_vma=False,
    )
```

```python
import jax
import jax.numpy as jnp
from jax import lax
from jax.experimental.layout import Layout, with_layout_constraint
from jax.sharding import PartitionSpec as P

STEPS = 2

SLOT_A = (3, 1, 1, 2)
SLOT_B = (2, 3, 3, 1)
LAST_P = (1, 2, 2, 3)
RIGHT = ((0, 1), (1, 2), (2, 3))
LEFT = ((3, 2), (2, 1), (1, 0))
LAST = ((0, 1), (1, 3), (3, 2), (2, 0))


def shifted(value, axis, steps):
    count = lax.axis_size(axis)
    pairs = [(source, (source + steps) % count) for source in range(count)]
    return lax.ppermute(value, axis, pairs)


def term(gathered, ket_p, bra_p, mpo_p):
    mixed = jnp.einsum(
        "wv,wba->vba", mpo_p, gathered, preferred_element_type=jnp.float32
    ).astype(jnp.bfloat16)
    rotated = jnp.einsum(
        "vba,ac->vbc", mixed, ket_p, preferred_element_type=jnp.float32
    ).astype(jnp.bfloat16)
    return jnp.einsum(
        "bd,vbc->vdc", bra_p, rotated, preferred_element_type=jnp.float32
    ).astype(jnp.bfloat16)


def chan_copies(piece):
    return [piece] + [shifted(piece, "chan", k) for k in range(1, lax.axis_size("chan"))]


def chan_gathered(pieces, mpo):
    count = lax.axis_size("chan")
    me = lax.axis_index("chan")
    held = [jnp.concatenate([p[k] for p in pieces], axis=0) for k in range(count)]
    width = held[0].shape[0]
    rows = [(me - k) % count for k in range(count)]
    order = jnp.concatenate([jnp.arange(width) + r * width for r in rows])
    return jnp.concatenate(held, axis=0), jnp.take(mpo, order, axis=0)


def pick(table, sector, ket, bra, mpo):
    p = jnp.asarray(table, jnp.int32)[sector]
    return (
        lax.dynamic_index_in_dim(ket, p, 0, keepdims=False),
        lax.dynamic_index_in_dim(bra, p, 0, keepdims=False),
        lax.dynamic_index_in_dim(mpo, p, 2, keepdims=False),
    )


def advance_line(current, ket, bra, mpo, live_mask, sector, held, pieces, finish):
    gathered, mpo = chan_gathered(current, mpo)
    f32 = jnp.float32
    one = jnp.ones((), f32)
    zero = jnp.zeros((), f32)
    slot_a = term(gathered, *pick(SLOT_A, sector, ket, bra, mpo))
    held, slot_a = lax.optimization_barrier((held, slot_a))
    got_right = lax.ppermute(slot_a, "sector", RIGHT)
    middle_left = lax.ppermute(slot_a, "sector", ((3, 1),))
    slot_b = term(gathered, *pick(SLOT_B, sector, ket, bra, mpo))
    got_left = lax.ppermute(slot_b, "sector", LEFT)
    middle_right = lax.ppermute(slot_b, "sector", ((0, 2),))
    third = term(gathered, *pick(LAST_P, sector, ket, bra, mpo))
    got = (got_right, got_left, middle_right, middle_left, third)
    got_right, got_left, middle_right, middle_left, third = lax.optimization_barrier(got)
    got_middle = middle_right + middle_left
    keep_right = jnp.where(sector == 1, zero, one)
    keep_left = jnp.where(sector == 2, zero, one)
    own = term(gathered, ket[0], bra[0], mpo[:, :, 0])
    total = own.astype(f32) + keep_right * got_right.astype(f32)
    total = total + keep_left * got_left.astype(f32) + got_middle.astype(f32)
    width = third.shape[0]
    bounds = [width * k // pieces for k in range(pieces + 1)]
    results = []
    piece = None
    for low, high in zip(bounds[:-1], bounds[1:]):
        send = third[low:high].astype(f32)
        send = send + (1 - keep_right) * got_right[low:high].astype(f32)
        send = send + (1 - keep_left) * got_left[low:high].astype(f32)
        send = send.astype(jnp.bfloat16)
        if results:
            piece, send = lax.optimization_barrier((piece, send))
            results[-1] = finish(piece)
        got_last = lax.ppermute(send, "sector", LAST)
        if results:
            results[-1], got_last = lax.optimization_barrier((results[-1], got_last))
        piece = total[low:high] + got_last.astype(f32)
        piece = (piece * live_mask[None]).astype(jnp.bfloat16)
        if finish is chan_copies:
            piece = with_layout_constraint(piece, Layout((0, 1, 2)))
        results.append(None)
    results[-1] = finish(piece)
    return results, held


def advance_direct(current, ket, bra, mpo, live_mask):
    stride = lax.axis_size("sector") // 2
    gathered, mpo = chan_gathered(current, mpo)
    f32 = jnp.float32
    total = term(gathered, ket[0], bra[0], mpo[:, :, 0]).astype(f32)
    for p, steps in ((1, 1), (2, stride), (3, stride + 1)):
        part = term(gathered, ket[p], bra[p], mpo[:, :, p])
        total = total + shifted(part, "sector", steps).astype(f32)
    return (total * live_mask[None]).astype(jnp.bfloat16)


def shards(environment, ket_tensor, bra_tensor, mpo_tensor, block_length):
    width = environment.shape[-1]
    index = jnp.arange(width, dtype=jnp.int32)
    alive = index < block_length[0]
    live_both = alive[:, None] & alive[None, :]
    live_mask = live_both.astype(jnp.float32)
    sector = lax.axis_index("sector")
    line = lax.axis_size("sector") == 4
    tensors = [(ket_tensor[0, 0], bra_tensor[0, 0], mpo_tensor[0])]
    for _ in range(1, STEPS):
        ket, bra, mpo = tensors[-1]
        tensors.append(tuple(shifted(t, "site", -1) for t in (ket, bra, mpo)))
    current = jnp.where(live_both, environment[0, :, 0], jnp.zeros((), jnp.bfloat16))
    def onward(part):
        return shifted(part[None, :, None], "site", STEPS)

    pieces = [chan_copies(current)]
    current = None
    for step in range(STEPS):
        ket, bra, mpo = tensors[step]
        last = step == STEPS - 1
        if line:
            parts, tensors[step + 1 :] = advance_line(
                pieces, ket, bra, mpo, live_mask, sector, tensors[step + 1 :],
                3 if last else 2, onward if last else chan_copies,
            )
        else:
            parts = [advance_direct(pieces, ket, bra, mpo, live_mask)]
            current = parts[0]
            parts = [onward(current)] if last else [chan_copies(current)]
        pieces = parts
    return jnp.concatenate(pieces, axis=1)


def solution(mesh):
    return jax.shard_map(
        shards,
        mesh=mesh,
        in_specs=(
            P("site", "chan", "sector", None, None),
            P("site", "sector", None, None, None),
            P("site", "sector", None, None, None),
            P("site", None, "chan", None),
            P("sector"),
        ),
        out_specs=P("site", "chan", "sector", None, None),
        check_vma=False,
    )
```

```python
import jax
import jax.numpy as jnp
from jax import lax
from jax.experimental.layout import Layout, with_layout_constraint
from jax.sharding import PartitionSpec as P

STEPS = 2

SLOT_A = (3, 1, 1, 2)
SLOT_B = (2, 3, 3, 1)
LAST_P = (1, 2, 2, 3)
RIGHT = ((0, 1), (1, 2), (2, 3))
LEFT = ((3, 2), (2, 1), (1, 0))
LAST = ((0, 1), (1, 3), (3, 2), (2, 0))


def shifted(value, axis, steps):
    count = lax.axis_size(axis)
    pairs = [(source, (source + steps) % count) for source in range(count)]
    return lax.ppermute(value, axis, pairs)


def term(gathered, ket_p, bra_p, mpo_p):
    mixed = jnp.einsum(
        "wv,wba->vba", mpo_p, gathered, preferred_element_type=jnp.float32
    ).astype(jnp.bfloat16)
    rotated = jnp.einsum(
        "vba,ac->vbc", mixed, ket_p, preferred_element_type=jnp.float32
    ).astype(jnp.bfloat16)
    return jnp.einsum(
        "bd,vbc->vdc", bra_p, rotated, preferred_element_type=jnp.float32
    ).astype(jnp.bfloat16)


def chan_copies(piece):
    return [piece] + [shifted(piece, "chan", k) for k in range(1, lax.axis_size("chan"))]


def chan_gathered(pieces, mpo):
    count = lax.axis_size("chan")
    me = lax.axis_index("chan")
    held = [jnp.concatenate([p[k] for p in pieces], axis=0) for k in range(count)]
    width = held[0].shape[0]
    rows = [(me - k) % count for k in range(count)]
    order = jnp.concatenate([jnp.arange(width) + r * width for r in rows])
    return jnp.concatenate(held, axis=0), jnp.take(mpo, order, axis=0)


def pick(table, sector, ket, bra, mpo):
    p = jnp.asarray(table, jnp.int32)[sector]
    return (
        lax.dynamic_index_in_dim(ket, p, 0, keepdims=False),
        lax.dynamic_index_in_dim(bra, p, 0, keepdims=False),
        lax.dynamic_index_in_dim(mpo, p, 2, keepdims=False),
    )


def advance_line(current, ket, bra, mpo, live_mask, sector, held, pieces, finish):
    gathered, mpo = chan_gathered(current, mpo)
    f32 = jnp.float32
    one = jnp.ones((), f32)
    zero = jnp.zeros((), f32)
    slot_a = term(gathered, *pick(SLOT_A, sector, ket, bra, mpo))
    held, slot_a = lax.optimization_barrier((held, slot_a))
    got_right = lax.ppermute(slot_a, "sector", RIGHT)
    middle_left = lax.ppermute(slot_a, "sector", ((3, 1),))
    slot_b = term(gathered, *pick(SLOT_B, sector, ket, bra, mpo))
    got_left = lax.ppermute(slot_b, "sector", LEFT)
    middle_right = lax.ppermute(slot_b, "sector", ((0, 2),))
    third = term(gathered, *pick(LAST_P, sector, ket, bra, mpo))
    got = (got_right, got_left, middle_right, middle_left, third)
    got_right, got_left, middle_right, middle_left, third = lax.optimization_barrier(got)
    got_middle = middle_right + middle_left
    keep_right = jnp.where(sector == 1, zero, one)
    keep_left = jnp.where(sector == 2, zero, one)
    own = term(gathered, ket[0], bra[0], mpo[:, :, 0])
    total = own.astype(f32) + keep_right * got_right.astype(f32)
    total = total + keep_left * got_left.astype(f32) + got_middle.astype(f32)
    width = third.shape[0]
    bounds = [width * k // pieces for k in range(pieces + 1)]
    results = []
    piece = None
    for low, high in zip(bounds[:-1], bounds[1:]):
        send = third[low:high].astype(f32)
        send = send + (1 - keep_right) * got_right[low:high].astype(f32)
        send = send + (1 - keep_left) * got_left[low:high].astype(f32)
        send = send.astype(jnp.bfloat16)
        if results:
            piece, send = lax.optimization_barrier((piece, send))
            results[-1] = finish(piece)
        got_last = lax.ppermute(send, "sector", LAST)
        if results:
            results[-1], got_last = lax.optimization_barrier((results[-1], got_last))
        piece = total[low:high] + got_last.astype(f32)
        piece = (piece * live_mask[None]).astype(jnp.bfloat16)
        if finish is chan_copies:
            piece = with_layout_constraint(piece, Layout((0, 1, 2)))
        results.append(None)
    results[-1] = finish(piece)
    return results, held


def advance_direct(current, ket, bra, mpo, live_mask):
    stride = lax.axis_size("sector") // 2
    gathered, mpo = chan_gathered(current, mpo)
    f32 = jnp.float32
    total = term(gathered, ket[0], bra[0], mpo[:, :, 0]).astype(f32)
    for p, steps in ((1, 1), (2, stride), (3, stride + 1)):
        part = term(gathered, ket[p], bra[p], mpo[:, :, p])
        total = total + shifted(part, "sector", steps).astype(f32)
    return (total * live_mask[None]).astype(jnp.bfloat16)


def shards(environment, ket_tensor, bra_tensor, mpo_tensor, block_length):
    width = environment.shape[-1]
    index = jnp.arange(width, dtype=jnp.int32)
    alive = index < block_length[0]
    live_both = alive[:, None] & alive[None, :]
    live_mask = live_both.astype(jnp.float32)
    sector = lax.axis_index("sector")
    line = lax.axis_size("sector") == 4
    tensors = [(ket_tensor[0, 0], bra_tensor[0, 0], mpo_tensor[0])]
    for _ in range(1, STEPS):
        ket, bra, mpo = tensors[-1]
        tensors.append(tuple(shifted(t, "site", -1) for t in (ket, bra, mpo)))
    def onward(part):
        return shifted(part[None, :, None], "site", STEPS)

    zero = jnp.zeros((), jnp.bfloat16)
    pieces = [[jnp.where(live_both, p, zero) for p in chan_copies(environment[0, :, 0])]]
    current = None
    for step in range(STEPS):
        ket, bra, mpo = tensors[step]
        last = step == STEPS - 1
        if line:
            parts, tensors[step + 1 :] = advance_line(
                pieces, ket, bra, mpo, live_mask, sector, tensors[step + 1 :],
                3 if last else 2, onward if last else chan_copies,
            )
        else:
            parts = [advance_direct(pieces, ket, bra, mpo, live_mask)]
            current = parts[0]
            parts = [onward(current)] if last else [chan_copies(current)]
        pieces = parts
    return jnp.concatenate(pieces, axis=1)


def solution(mesh):
    return jax.shard_map(
        shards,
        mesh=mesh,
        in_specs=(
            P("site", "chan", "sector", None, None),
            P("site", "sector", None, None, None),
            P("site", "sector", None, None, None),
            P("site", None, "chan", None),
            P("sector"),
        ),
        out_specs=P("site", "chan", "sector", None, None),
        check_vma=False,
    )
```

```python
import jax
import jax.numpy as jnp
from jax import lax
from jax.experimental.layout import Layout, with_layout_constraint
from jax.sharding import PartitionSpec as P

STEPS = 2

SLOT_A = (3, 1, 1, 2)
SLOT_B = (2, 3, 3, 1)
LAST_P = (1, 2, 2, 3)
RIGHT = ((0, 1), (1, 2), (2, 3))
LEFT = ((3, 2), (2, 1), (1, 0))
LAST = ((0, 1), (1, 3), (3, 2), (2, 0))


def shifted(value, axis, steps):
    count = lax.axis_size(axis)
    pairs = [(source, (source + steps) % count) for source in range(count)]
    return lax.ppermute(value, axis, pairs)


def term(gathered, ket_p, bra_p, mpo_p):
    mixed = jnp.einsum(
        "wv,wba->vba", mpo_p, gathered, preferred_element_type=jnp.float32
    ).astype(jnp.bfloat16)
    rotated = jnp.einsum(
        "vba,ac->vbc", mixed, ket_p, preferred_element_type=jnp.float32
    ).astype(jnp.bfloat16)
    return jnp.einsum(
        "bd,vbc->vdc", bra_p, rotated, preferred_element_type=jnp.float32
    ).astype(jnp.bfloat16)


def chan_copies(piece):
    return [piece] + [shifted(piece, "chan", k) for k in range(1, lax.axis_size("chan"))]


def chan_gathered(pieces, mpo):
    count = lax.axis_size("chan")
    me = lax.axis_index("chan")
    held = [jnp.concatenate([p[k] for p in pieces], axis=0) for k in range(count)]
    width = held[0].shape[0]
    rows = [(me - k) % count for k in range(count)]
    order = jnp.concatenate([jnp.arange(width) + r * width for r in rows])
    return jnp.concatenate(held, axis=0), jnp.take(mpo, order, axis=0)


def pick(table, sector, ket, bra, mpo):
    p = jnp.asarray(table, jnp.int32)[sector]
    return (
        lax.dynamic_index_in_dim(ket, p, 0, keepdims=False),
        lax.dynamic_index_in_dim(bra, p, 0, keepdims=False),
        lax.dynamic_index_in_dim(mpo, p, 2, keepdims=False),
    )


def advance_line(current, ket, bra, mpo, live_mask, sector, held, pieces, finish):
    gathered, mpo = chan_gathered(current, mpo)
    f32 = jnp.float32
    one = jnp.ones((), f32)
    zero = jnp.zeros((), f32)
    slot_a = term(gathered, *pick(SLOT_A, sector, ket, bra, mpo))
    held, slot_a = lax.optimization_barrier((held, slot_a))
    got_right = lax.ppermute(slot_a, "sector", RIGHT)
    middle_left = lax.ppermute(slot_a, "sector", ((3, 1),))
    slot_b = term(gathered, *pick(SLOT_B, sector, ket, bra, mpo))
    got_left = lax.ppermute(slot_b, "sector", LEFT)
    middle_right = lax.ppermute(slot_b, "sector", ((0, 2),))
    third = term(gathered, *pick(LAST_P, sector, ket, bra, mpo))
    got = (got_right, got_left, middle_right, middle_left, third)
    got_right, got_left, middle_right, middle_left, third = lax.optimization_barrier(got)
    got_middle = middle_right + middle_left
    keep_right = jnp.where(sector == 1, zero, one)
    keep_left = jnp.where(sector == 2, zero, one)
    own = term(gathered, ket[0], bra[0], mpo[:, :, 0])
    total = own.astype(f32) + keep_right * got_right.astype(f32)
    total = total + keep_left * got_left.astype(f32) + got_middle.astype(f32)
    width = third.shape[0]
    bounds = [width * k // pieces for k in range(pieces + 1)]
    results = []
    piece = None
    for low, high in zip(bounds[:-1], bounds[1:]):
        send = third[low:high].astype(f32)
        send = send + (1 - keep_right) * got_right[low:high].astype(f32)
        send = send + (1 - keep_left) * got_left[low:high].astype(f32)
        send = send.astype(jnp.bfloat16)
        if results:
            piece, send = lax.optimization_barrier((piece, send))
            results[-1] = finish(piece)
        got_last = lax.ppermute(send, "sector", LAST)
        if results:
            results[-1], got_last = lax.optimization_barrier((results[-1], got_last))
        piece = total[low:high] + got_last.astype(f32)
        piece = (piece * live_mask[None]).astype(jnp.bfloat16)
        if finish is chan_copies:
            piece = with_layout_constraint(piece, Layout((0, 1, 2)))
        results.append(None)
    results[-1] = finish(piece)
    return results, held


def advance_direct(current, ket, bra, mpo, live_mask):
    stride = lax.axis_size("sector") // 2
    gathered, mpo = chan_gathered(current, mpo)
    f32 = jnp.float32
    total = term(gathered, ket[0], bra[0], mpo[:, :, 0]).astype(f32)
    for p, steps in ((1, 1), (2, stride), (3, stride + 1)):
        part = term(gathered, ket[p], bra[p], mpo[:, :, p])
        total = total + shifted(part, "sector", steps).astype(f32)
    return (total * live_mask[None]).astype(jnp.bfloat16)


def shards(environment, ket_tensor, bra_tensor, mpo_tensor, block_length):
    width = environment.shape[-1]
    index = jnp.arange(width, dtype=jnp.int32)
    alive = index < block_length[0]
    live_both = alive[:, None] & alive[None, :]
    live_mask = live_both.astype(jnp.float32)
    sector = lax.axis_index("sector")
    line = lax.axis_size("sector") == 4
    tensors = [(ket_tensor[0, 0], bra_tensor[0, 0], mpo_tensor[0])]
    for _ in range(1, STEPS):
        ket, bra, mpo = tensors[-1]
        both = shifted(jnp.concatenate([ket, bra]), "site", -1)
        tensors.append((both[: ket.shape[0]], both[ket.shape[0] :], shifted(mpo, "site", -1)))
    current = jnp.where(live_both, environment[0, :, 0], jnp.zeros((), jnp.bfloat16))
    def onward(part):
        return shifted(part[None, :, None], "site", STEPS)

    pieces = [chan_copies(current)]
    current = None
    for step in range(STEPS):
        ket, bra, mpo = tensors[step]
        last = step == STEPS - 1
        if line:
            parts, tensors[step + 1 :] = advance_line(
                pieces, ket, bra, mpo, live_mask, sector, tensors[step + 1 :],
                3 if last else 2, onward if last else chan_copies,
            )
        else:
            parts = [advance_direct(pieces, ket, bra, mpo, live_mask)]
            current = parts[0]
            parts = [onward(current)] if last else [chan_copies(current)]
        pieces = parts
    return jnp.concatenate(pieces, axis=1)


def solution(mesh):
    return jax.shard_map(
        shards,
        mesh=mesh,
        in_specs=(
            P("site", "chan", "sector", None, None),
            P("site", "sector", None, None, None),
            P("site", "sector", None, None, None),
            P("site", None, "chan", None),
            P("sector"),
        ),
        out_specs=P("site", "chan", "sector", None, None),
        check_vma=False,
    )
```

```python
import jax
import jax.numpy as jnp
from jax import lax
from jax.experimental.layout import Layout, with_layout_constraint
from jax.sharding import PartitionSpec as P

STEPS = 2

SLOT_A = (3, 1, 1, 2)
SLOT_B = (2, 3, 3, 1)
LAST_P = (1, 2, 2, 3)
RIGHT = ((0, 1), (1, 2), (2, 3))
LEFT = ((3, 2), (2, 1), (1, 0))
LAST = ((0, 1), (1, 3), (3, 2), (2, 0))


def shifted(value, axis, steps):
    count = lax.axis_size(axis)
    pairs = [(source, (source + steps) % count) for source in range(count)]
    return lax.ppermute(value, axis, pairs)


def term(gathered, ket_p, bra_p, mpo_p):
    mixed = jnp.einsum(
        "wv,wba->vba", mpo_p, gathered, preferred_element_type=jnp.float32
    ).astype(jnp.bfloat16)
    rotated = jnp.einsum(
        "vba,ac->vbc", mixed, ket_p, preferred_element_type=jnp.float32
    ).astype(jnp.bfloat16)
    return jnp.einsum(
        "bd,vbc->vdc", bra_p, rotated, preferred_element_type=jnp.float32
    ).astype(jnp.bfloat16)


def chan_copies(piece):
    return [piece] + [shifted(piece, "chan", k) for k in range(1, lax.axis_size("chan"))]


def chan_gathered(pieces, mpo):
    count = lax.axis_size("chan")
    me = lax.axis_index("chan")
    held = [jnp.concatenate([p[k] for p in pieces], axis=0) for k in range(count)]
    width = held[0].shape[0]
    rows = [(me - k) % count for k in range(count)]
    order = jnp.concatenate([jnp.arange(width) + r * width for r in rows])
    return jnp.concatenate(held, axis=0), jnp.take(mpo, order, axis=0)


def pick(table, sector, ket, bra, mpo):
    p = jnp.asarray(table, jnp.int32)[sector]
    return (
        lax.dynamic_index_in_dim(ket, p, 0, keepdims=False),
        lax.dynamic_index_in_dim(bra, p, 0, keepdims=False),
        lax.dynamic_index_in_dim(mpo, p, 2, keepdims=False),
    )


def advance_line(current, ket, bra, mpo, live_mask, sector, held, pieces, finish):
    gathered, mpo = chan_gathered(current, mpo)
    f32 = jnp.float32
    one = jnp.ones((), f32)
    zero = jnp.zeros((), f32)
    slot_a = term(gathered, *pick(SLOT_A, sector, ket, bra, mpo))
    held, slot_a = lax.optimization_barrier((held, slot_a))
    got_right = lax.ppermute(slot_a, "sector", RIGHT)
    middle_left = lax.ppermute(slot_a, "sector", ((3, 1),))
    slot_b = term(gathered, *pick(SLOT_B, sector, ket, bra, mpo))
    got_left = lax.ppermute(slot_b, "sector", LEFT)
    middle_right = lax.ppermute(slot_b, "sector", ((0, 2),))
    third = term(gathered, *pick(LAST_P, sector, ket, bra, mpo))
    got = (got_right, got_left, middle_right, middle_left, third)
    got_right, got_left, middle_right, middle_left, third = lax.optimization_barrier(got)
    got_middle = middle_right + middle_left
    keep_right = jnp.where(sector == 1, zero, one)
    keep_left = jnp.where(sector == 2, zero, one)
    own = term(gathered, ket[0], bra[0], mpo[:, :, 0])
    total = own.astype(f32) + keep_right * got_right.astype(f32)
    total = total + keep_left * got_left.astype(f32) + got_middle.astype(f32)
    width = third.shape[0]
    bounds = [width * k // pieces for k in range(pieces + 1)]
    if finish is not chan_copies:
        weights = [sum(range(pieces, pieces - k, -1)) for k in range(pieces + 1)]
        bounds = [width * w // weights[-1] for w in weights]
    results = []
    piece = None
    for low, high in zip(bounds[:-1], bounds[1:]):
        send = third[low:high].astype(f32)
        send = send + (1 - keep_right) * got_right[low:high].astype(f32)
        send = send + (1 - keep_left) * got_left[low:high].astype(f32)
        send = send.astype(jnp.bfloat16)
        if results:
            piece, send = lax.optimization_barrier((piece, send))
            results[-1] = finish(piece)
        got_last = lax.ppermute(send, "sector", LAST)
        if results:
            results[-1], got_last = lax.optimization_barrier((results[-1], got_last))
        piece = total[low:high] + got_last.astype(f32)
        piece = (piece * live_mask[None]).astype(jnp.bfloat16)
        if finish is chan_copies:
            piece = with_layout_constraint(piece, Layout((0, 1, 2)))
        results.append(None)
    results[-1] = finish(piece)
    return results, held


def advance_direct(current, ket, bra, mpo, live_mask):
    stride = lax.axis_size("sector") // 2
    gathered, mpo = chan_gathered(current, mpo)
    f32 = jnp.float32
    total = term(gathered, ket[0], bra[0], mpo[:, :, 0]).astype(f32)
    for p, steps in ((1, 1), (2, stride), (3, stride + 1)):
        part = term(gathered, ket[p], bra[p], mpo[:, :, p])
        total = total + shifted(part, "sector", steps).astype(f32)
    return (total * live_mask[None]).astype(jnp.bfloat16)


def shards(environment, ket_tensor, bra_tensor, mpo_tensor, block_length):
    width = environment.shape[-1]
    index = jnp.arange(width, dtype=jnp.int32)
    alive = index < block_length[0]
    live_both = alive[:, None] & alive[None, :]
    live_mask = live_both.astype(jnp.float32)
    sector = lax.axis_index("sector")
    line = lax.axis_size("sector") == 4
    tensors = [(ket_tensor[0, 0], bra_tensor[0, 0], mpo_tensor[0])]
    for _ in range(1, STEPS):
        ket, bra, mpo = tensors[-1]
        tensors.append(tuple(shifted(t, "site", -1) for t in (ket, bra, mpo)))
    current = jnp.where(live_both, environment[0, :, 0], jnp.zeros((), jnp.bfloat16))
    def onward(part):
        return shifted(part[None, :, None], "site", STEPS)

    pieces = [chan_copies(current)]
    current = None
    for step in range(STEPS):
        ket, bra, mpo = tensors[step]
        last = step == STEPS - 1
        if line:
            parts, tensors[step + 1 :] = advance_line(
                pieces, ket, bra, mpo, live_mask, sector, tensors[step + 1 :],
                3 if last else 2, onward if last else chan_copies,
            )
        else:
            parts = [advance_direct(pieces, ket, bra, mpo, live_mask)]
            current = parts[0]
            parts = [onward(current)] if last else [chan_copies(current)]
        pieces = parts
    return jnp.concatenate(pieces, axis=1)


def solution(mesh):
    return jax.shard_map(
        shards,
        mesh=mesh,
        in_specs=(
            P("site", "chan", "sector", None, None),
            P("site", "sector", None, None, None),
            P("site", "sector", None, None, None),
            P("site", None, "chan", None),
            P("sector"),
        ),
        out_specs=P("site", "chan", "sector", None, None),
        check_vma=False,
    )
```

```python
import jax
import jax.numpy as jnp
from jax import lax
from jax.experimental.layout import Layout, with_layout_constraint
from jax.sharding import PartitionSpec as P

STEPS = 2

SLOT_A = (3, 1, 1, 2)
SLOT_B = (2, 3, 3, 1)
LAST_P = (1, 2, 2, 3)
RIGHT = ((0, 1), (1, 2), (2, 3))
LEFT = ((3, 2), (2, 1), (1, 0))
LAST = ((0, 1), (1, 3), (3, 2), (2, 0))


def shifted(value, axis, steps):
    count = lax.axis_size(axis)
    pairs = [(source, (source + steps) % count) for source in range(count)]
    return lax.ppermute(value, axis, pairs)


def term(gathered, ket_p, bra_p, mpo_p):
    mixed = jnp.einsum(
        "wv,wba->vba", mpo_p, gathered, preferred_element_type=jnp.float32
    ).astype(jnp.bfloat16)
    rotated = jnp.einsum(
        "vba,ac->vbc", mixed, ket_p, preferred_element_type=jnp.float32
    ).astype(jnp.bfloat16)
    return jnp.einsum(
        "bd,vbc->vdc", bra_p, rotated, preferred_element_type=jnp.float32
    ).astype(jnp.bfloat16)


def chan_copies(piece):
    return [piece] + [shifted(piece, "chan", k) for k in range(1, lax.axis_size("chan"))]


def chan_gathered(pieces, mpo):
    count = lax.axis_size("chan")
    me = lax.axis_index("chan")
    held = [jnp.concatenate([p[k] for p in pieces], axis=0) for k in range(count)]
    width = held[0].shape[0]
    rows = [(me - k) % count for k in range(count)]
    order = jnp.concatenate([jnp.arange(width) + r * width for r in rows])
    return jnp.concatenate(held, axis=0), jnp.take(mpo, order, axis=0)


def pick(table, sector, ket, bra, mpo):
    p = jnp.asarray(table, jnp.int32)[sector]
    return (
        lax.dynamic_index_in_dim(ket, p, 0, keepdims=False),
        lax.dynamic_index_in_dim(bra, p, 0, keepdims=False),
        lax.dynamic_index_in_dim(mpo, p, 2, keepdims=False),
    )


def advance_line(current, ket, bra, mpo, live_mask, sector, held, pieces, finish):
    gathered, mpo = chan_gathered(current, mpo)
    f32 = jnp.float32
    one = jnp.ones((), f32)
    zero = jnp.zeros((), f32)
    slot_a = term(gathered, *pick(SLOT_A, sector, ket, bra, mpo))
    held, slot_a = lax.optimization_barrier((held, slot_a))
    got_right = lax.ppermute(slot_a, "sector", RIGHT)
    middle_left = lax.ppermute(slot_a, "sector", ((3, 1),))
    slot_b = term(gathered, *pick(SLOT_B, sector, ket, bra, mpo))
    got_left = lax.ppermute(slot_b, "sector", LEFT)
    middle_right = lax.ppermute(slot_b, "sector", ((0, 2),))
    third = term(gathered, *pick(LAST_P, sector, ket, bra, mpo))
    got = (got_right, got_left, middle_right, middle_left, third)
    got_right, got_left, middle_right, middle_left, third = lax.optimization_barrier(got)
    got_middle = middle_right + middle_left
    keep_right = jnp.where(sector == 1, zero, one)
    keep_left = jnp.where(sector == 2, zero, one)
    own = term(gathered, ket[0], bra[0], mpo[:, :, 0])
    total = own.astype(f32) + keep_right * got_right.astype(f32)
    total = total + keep_left * got_left.astype(f32) + got_middle.astype(f32)
    width = third.shape[0]
    bounds = [width - width * (pieces - k) // pieces for k in range(pieces + 1)]
    if finish is not chan_copies:
        weights = [sum(range(pieces, pieces - k, -1)) for k in range(pieces + 1)]
        bounds = [width * w // weights[-1] for w in weights]
    results = []
    piece = None
    for low, high in zip(bounds[:-1], bounds[1:]):
        send = third[low:high].astype(f32)
        send = send + (1 - keep_right) * got_right[low:high].astype(f32)
        send = send + (1 - keep_left) * got_left[low:high].astype(f32)
        send = send.astype(jnp.bfloat16)
        if results:
            piece, send = lax.optimization_barrier((piece, send))
            results[-1] = finish(piece)
        got_last = lax.ppermute(send, "sector", LAST)
        if results:
            results[-1], got_last = lax.optimization_barrier((results[-1], got_last))
        piece = total[low:high] + got_last.astype(f32)
        piece = (piece * live_mask[None]).astype(jnp.bfloat16)
        if finish is chan_copies:
            piece = with_layout_constraint(piece, Layout((0, 1, 2)))
        results.append(None)
    results[-1] = finish(piece)
    return results, held


def advance_direct(current, ket, bra, mpo, live_mask):
    stride = lax.axis_size("sector") // 2
    gathered, mpo = chan_gathered(current, mpo)
    f32 = jnp.float32
    total = term(gathered, ket[0], bra[0], mpo[:, :, 0]).astype(f32)
    for p, steps in ((1, 1), (2, stride), (3, stride + 1)):
        part = term(gathered, ket[p], bra[p], mpo[:, :, p])
        total = total + shifted(part, "sector", steps).astype(f32)
    return (total * live_mask[None]).astype(jnp.bfloat16)


def shards(environment, ket_tensor, bra_tensor, mpo_tensor, block_length):
    width = environment.shape[-1]
    index = jnp.arange(width, dtype=jnp.int32)
    alive = index < block_length[0]
    live_both = alive[:, None] & alive[None, :]
    live_mask = live_both.astype(jnp.float32)
    sector = lax.axis_index("sector")
    line = lax.axis_size("sector") == 4
    tensors = [(ket_tensor[0, 0], bra_tensor[0, 0], mpo_tensor[0])]
    for _ in range(1, STEPS):
        ket, bra, mpo = tensors[-1]
        tensors.append(tuple(shifted(t, "site", -1) for t in (ket, bra, mpo)))
    current = jnp.where(live_both, environment[0, :, 0], jnp.zeros((), jnp.bfloat16))
    def onward(part):
        return shifted(part[None, :, None], "site", STEPS)

    pieces = [chan_copies(current)]
    current = None
    for step in range(STEPS):
        ket, bra, mpo = tensors[step]
        last = step == STEPS - 1
        if line:
            parts, tensors[step + 1 :] = advance_line(
                pieces, ket, bra, mpo, live_mask, sector, tensors[step + 1 :],
                3 if last else 2, onward if last else chan_copies,
            )
        else:
            parts = [advance_direct(pieces, ket, bra, mpo, live_mask)]
            current = parts[0]
            parts = [onward(current)] if last else [chan_copies(current)]
        pieces = parts
    return jnp.concatenate(pieces, axis=1)


def solution(mesh):
    return jax.shard_map(
        shards,
        mesh=mesh,
        in_specs=(
            P("site", "chan", "sector", None, None),
            P("site", "sector", None, None, None),
            P("site", "sector", None, None, None),
            P("site", None, "chan", None),
            P("sector"),
        ),
        out_specs=P("site", "chan", "sector", None, None),
        check_vma=False,
    )
```

```python
import jax
import jax.numpy as jnp
from jax import lax
from jax.experimental.layout import Layout, with_layout_constraint
from jax.sharding import PartitionSpec as P

STEPS = 2

SLOT_A = (3, 1, 1, 2)
SLOT_B = (2, 3, 3, 1)
LAST_P = (1, 2, 2, 3)
RIGHT = ((0, 1), (1, 2), (2, 3))
LEFT = ((3, 2), (2, 1), (1, 0))
LAST = ((0, 1), (1, 3), (3, 2), (2, 0))


def shifted(value, axis, steps):
    count = lax.axis_size(axis)
    pairs = [(source, (source + steps) % count) for source in range(count)]
    return lax.ppermute(value, axis, pairs)


def term(gathered, ket_p, bra_p, mpo_p):
    mixed = jnp.einsum(
        "wv,wba->vba", mpo_p, gathered, preferred_element_type=jnp.float32
    ).astype(jnp.bfloat16)
    rotated = jnp.einsum(
        "vba,ac->vbc", mixed, ket_p, preferred_element_type=jnp.float32
    ).astype(jnp.bfloat16)
    return jnp.einsum(
        "bd,vbc->vdc", bra_p, rotated, preferred_element_type=jnp.float32
    ).astype(jnp.bfloat16)


def chan_copies(piece):
    return [piece] + [shifted(piece, "chan", k) for k in range(1, lax.axis_size("chan"))]


def chan_gathered(pieces, mpo):
    count = lax.axis_size("chan")
    me = lax.axis_index("chan")
    held = [jnp.concatenate([p[k] for p in pieces], axis=0) for k in range(count)]
    width = held[0].shape[0]
    rows = [(me - k) % count for k in range(count)]
    order = jnp.concatenate([jnp.arange(width) + r * width for r in rows])
    return jnp.concatenate(held, axis=0), jnp.take(mpo, order, axis=0)


def pick(table, sector, ket, bra, mpo):
    p = jnp.asarray(table, jnp.int32)[sector]
    return (
        lax.dynamic_index_in_dim(ket, p, 0, keepdims=False),
        lax.dynamic_index_in_dim(bra, p, 0, keepdims=False),
        lax.dynamic_index_in_dim(mpo, p, 2, keepdims=False),
    )


def advance_line(current, ket, bra, mpo, live_mask, sector, held, pieces, finish):
    gathered, mpo = chan_gathered(current, mpo)
    f32 = jnp.float32
    one = jnp.ones((), f32)
    zero = jnp.zeros((), f32)
    slot_a = term(gathered, *pick(SLOT_A, sector, ket, bra, mpo))
    held, slot_a = lax.optimization_barrier((held, slot_a))
    got_right = lax.ppermute(slot_a, "sector", RIGHT)
    middle_left = lax.ppermute(slot_a, "sector", ((3, 1),))
    slot_b = term(gathered, *pick(SLOT_B, sector, ket, bra, mpo))
    got_left = lax.ppermute(slot_b, "sector", LEFT)
    middle_right = lax.ppermute(slot_b, "sector", ((0, 2),))
    third = term(gathered, *pick(LAST_P, sector, ket, bra, mpo))
    got = (got_right, got_left, middle_right, middle_left, third)
    got_right, got_left, middle_right, middle_left, third = lax.optimization_barrier(got)
    got_middle = middle_right + middle_left
    keep_right = jnp.where(sector == 1, zero, one)
    keep_left = jnp.where(sector == 2, zero, one)
    own = term(gathered, ket[0], bra[0], mpo[:, :, 0])
    total = own.astype(f32) + keep_right * got_right.astype(f32)
    total = total + keep_left * got_left.astype(f32) + got_middle.astype(f32)
    width = third.shape[0]
    bounds = [width * k // pieces for k in range(pieces + 1)]
    if finish is not chan_copies:
        weights = [sum(range(pieces, pieces - k, -1)) for k in range(pieces + 1)]
        bounds = [width * w // weights[-1] for w in weights]
    results = []
    piece = None
    for low, high in zip(bounds[:-1], bounds[1:]):
        send = third[low:high].astype(f32)
        send = send + (1 - keep_right) * got_right[low:high].astype(f32)
        send = send + (1 - keep_left) * got_left[low:high].astype(f32)
        send = send.astype(jnp.bfloat16)
        if results:
            piece, send = lax.optimization_barrier((piece, send))
            results[-1] = finish(piece)
        got_last = lax.ppermute(send, "sector", LAST)
        if results:
            results[-1], got_last = lax.optimization_barrier((results[-1], got_last))
        piece = total[low:high] + got_last.astype(f32)
        piece = (piece * live_mask[None]).astype(jnp.bfloat16)
        if finish is chan_copies:
            piece = with_layout_constraint(piece, Layout((0, 1, 2)))
        results.append(None)
    results[-1] = finish(piece)
    return results, held


def advance_direct(current, ket, bra, mpo, live_mask):
    stride = lax.axis_size("sector") // 2
    gathered, mpo = chan_gathered(current, mpo)
    f32 = jnp.float32
    total = term(gathered, ket[0], bra[0], mpo[:, :, 0]).astype(f32)
    for p, steps in ((1, 1), (2, stride), (3, stride + 1)):
        part = term(gathered, ket[p], bra[p], mpo[:, :, p])
        total = total + shifted(part, "sector", steps).astype(f32)
    return (total * live_mask[None]).astype(jnp.bfloat16)


def shards(environment, ket_tensor, bra_tensor, mpo_tensor, block_length):
    width = environment.shape[-1]
    index = jnp.arange(width, dtype=jnp.int32)
    alive = index < block_length[0]
    live_both = alive[:, None] & alive[None, :]
    live_mask = live_both.astype(jnp.float32)
    sector = lax.axis_index("sector")
    line = lax.axis_size("sector") == 4
    tensors = [(ket_tensor[0, 0], bra_tensor[0, 0], mpo_tensor[0])]
    for _ in range(1, STEPS):
        ket, bra, mpo = tensors[-1]
        tensors.append(tuple(shifted(t, "site", -1) for t in (ket, bra, mpo)))
    current = jnp.where(live_both, environment[0, :, 0], jnp.zeros((), jnp.bfloat16))
    def onward(part):
        return shifted(part[None, :, None], "site", STEPS)

    pieces = [chan_copies(current)]
    current = None
    for step in range(STEPS):
        ket, bra, mpo = tensors[step]
        last = step == STEPS - 1
        if line:
            parts, tensors[step + 1 :] = advance_line(
                pieces, ket, bra, mpo, live_mask, sector, tensors[step + 1 :],
                4 if last else 2, onward if last else chan_copies,
            )
        else:
            parts = [advance_direct(pieces, ket, bra, mpo, live_mask)]
            current = parts[0]
            parts = [onward(current)] if last else [chan_copies(current)]
        pieces = parts
    return jnp.concatenate(pieces, axis=1)


def solution(mesh):
    return jax.shard_map(
        shards,
        mesh=mesh,
        in_specs=(
            P("site", "chan", "sector", None, None),
            P("site", "sector", None, None, None),
            P("site", "sector", None, None, None),
            P("site", None, "chan", None),
            P("sector"),
        ),
        out_specs=P("site", "chan", "sector", None, None),
        check_vma=False,
    )
```
